512 devices in a mesh: seq: 64 (over z, y), head: 8 (over x, core).
Axes of the slice: x: 4, y: 8, z: 8, core: 2. Of those that a mesh axis runs over, the one named last changes fastest.
Arguments:
- queries: bfloat16 [2, 4096, 8192], P(None, 'seq', 'head'), may hold values from -10 to 10
- key_states: bfloat16 [2, 4096, 1024], P(None, ('seq', 'head')), may hold values from -10 to 10
- value_state_rows: bfloat16 [2, 4096, 1024], P(None, ('seq', 'head')), may hold values from -6 to 6
- grad_out: bfloat16 [2, 4096, 8192], P(None, 'seq', 'head'), may hold values from -6 to 6
- layouts: int32 [4, 128, 8], replicated, may hold values from 0 to 127, as said below
- plant_ids: int32 [128], replicated, may hold values from 0 to 3
Outputs:
- attended: bfloat16 [2, 4096, 8192], P(None, 'seq', 'head')
- query_grad: bfloat16 [2, 4096, 8192], P(None, 'seq', 'head')
- key_grad: bfloat16 [2, 4096, 1024], P(None, ('seq', 'head'))
- value_grad: bfloat16 [2, 4096, 1024], P(None, ('seq', 'head'))
The draws below stay inside these ranges and needn't reach their ends.
Inputs may be any that keep to these rules, and one draw needn't show every extreme that they name: Entry 0 of layouts[p, q] is q and every entry is at most q. With owner(b) = b for b < 64 and 127 - b otherwise: if an entry b of layouts[p, q] has owner(b) = o other than owner(q) = d, then b = o when o < d and b = 127 - o when o > d.
All inputs are finite; a program needn't handle non-finite values.
Results may differ from the reference program's by a relative error of at most 0.011.
Values may be sent and summed in bfloat16 or wider, within the bound.
No kernel may reach another device: no remote copies, remote signals or barrier semaphores. Data moves between devices by JAX's collectives and lax.ppermute only.
A program may use at most 64 MiB of HBM per device.

```python
import jax
import jax.numpy as jnp
from jax import lax

QUERY_HEADS_N = 64
KEY_VALUE_HEADS = 8
HEAD_SIZE = 128
BLOCK_TOKENS_N = 64
KEY_LIST_SIZE = 8
PLANTS = 4
SEQUENCE_BLOCKS = 128


def draw_queries(key, part):
    random_noise = jax.random.normal(jax.random.fold_in(key, 1), (2, SEQUENCE_BLOCKS // 2, BLOCK_TOKENS_N, QUERY_HEADS_N * HEAD_SIZE), jnp.float32)
    random_noise = jnp.clip(random_noise, -8.0, 8.0)
    return random_noise.reshape(2, SEQUENCE_BLOCKS // 2 * BLOCK_TOKENS_N, QUERY_HEADS_N * HEAD_SIZE).astype(jnp.bfloat16)


def draw_key_states(key, part):
    random_noise = jax.random.normal(jax.random.fold_in(key, 2), (2, SEQUENCE_BLOCKS // 2, BLOCK_TOKENS_N, KEY_VALUE_HEADS * HEAD_SIZE), jnp.float32)
    random_noise = jnp.clip(random_noise, -8.0, 8.0)
    return random_noise.reshape(2, SEQUENCE_BLOCKS // 2 * BLOCK_TOKENS_N, KEY_VALUE_HEADS * HEAD_SIZE).astype(jnp.bfloat16)


def draw_layouts(key, part):
    halfway = SEQUENCE_BLOCKS // 2
    blocks = jnp.arange(SEQUENCE_BLOCKS, dtype=jnp.int32)
    owner = jnp.where(blocks < halfway, blocks, SEQUENCE_BLOCKS - 1 - blocks)
    limit = jnp.where(blocks < halfway, owner + 1, halfway)
    base_key = jax.random.fold_in(key, 11)
    first_key, second_key, third_key = jax.random.split(base_key, 3)
    popular = jax.random.randint(first_key, (PLANTS, 4), 0, halfway)
    which_one = jax.random.randint(third_key, (PLANTS, SEQUENCE_BLOCKS), 0, 4)
    choices_four = jnp.arange(4, dtype=jnp.int32)
    popular_peer = jnp.sum(jnp.where(which_one[:, :, None] == choices_four[None, None, :], popular[:, None, :], 0), axis=-1)
    raw_draw = jax.random.randint(second_key, (PLANTS, SEQUENCE_BLOCKS, KEY_LIST_SIZE), 0, 1 << 20)
    peers = raw_draw % limit[None, :, None]
    peers = peers.at[:, :, 2].set(popular_peer)
    owner_b = owner[None, :, None]
    lower_query = (blocks < halfway)[None, :, None]
    peers = jnp.where(lower_query, jnp.minimum(peers, owner_b), peers)
    chosen = jnp.where(peers == owner_b, blocks[None, :, None], jnp.where(peers < owner_b, peers, SEQUENCE_BLOCKS - 1 - peers))
    previous = jnp.maximum(blocks - 1, 0)
    chosen = chosen.at[:, :, 0].set(jnp.broadcast_to(blocks[None, :], (PLANTS, SEQUENCE_BLOCKS)))
    chosen = chosen.at[:, :, 1].set(jnp.broadcast_to(previous[None, :], (PLANTS, SEQUENCE_BLOCKS)))
    return chosen.astype(jnp.int32)


def plant(result, stream_key, low, largest):
    shape = result.shape
    index_at = [jax.random.randint(jax.random.fold_in(stream_key, axis), (), 0, shape[axis]) for axis in range(len(shape))]
    result = result.at[tuple(index_at)].set(low)
    longest = shape.index(max(shape))
    index_at[longest] = (index_at[longest] + 1) % shape[longest]
    return result.at[tuple(index_at)].set(largest)


def block_scale(own_key, extent, cuts, low, top_value):
    gain, own = 1.0, jax.random.fold_in(own_key, 6)
    for position, shards_of in cuts:
        heights = jnp.exp(jax.random.uniform(jax.random.fold_in(own, position), (shards_of,), jnp.float32, low / len(cuts), top_value / len(cuts)))
        gain = gain * jnp.repeat(heights, extent[position] // shards_of).reshape([-1 if axis == position else 1 for axis in range(len(extent))])
    return gain


def bell_draw(own_key, shape, deviation, reach, cuts=(), kind=jnp.bfloat16):
    values = jax.random.normal(own_key, shape, jnp.float32) * deviation
    if len(cuts) > 0:
        values = block_scale(own_key, shape, cuts, -0.22, 0.18) * values
    return jnp.clip(values, min=-reach, max=reach).astype(kind)


def setup_inputs(seed: int = 0) -> dict:
    key_of = jax.random.split(jax.random.key(seed), 7)
    return {
        "queries": draw_queries(jax.random.fold_in(key_of[6], 71), 0),
        "key_states": draw_key_states(jax.random.fold_in(key_of[6], 71), 0),
        "value_state_rows": bell_draw(key_of[2], (2, SEQUENCE_BLOCKS // 2 * BLOCK_TOKENS_N, KEY_VALUE_HEADS * HEAD_SIZE), 1.0, 6.0, ((1, 512),)),
        "grad_out": bell_draw(key_of[3], (2, SEQUENCE_BLOCKS // 2 * BLOCK_TOKENS_N, QUERY_HEADS_N * HEAD_SIZE), 1.0, 6.0, ((1, 64), (2, 8))),
        "layouts": draw_layouts(jax.random.fold_in(key_of[6], 71), 0),
        "plant_ids": plant(jax.random.randint(key_of[5], (SEQUENCE_BLOCKS,), 0, PLANTS), jax.random.fold_in(key_of[5], 1), 0, PLANTS - 1).astype(jnp.int32),
    }


def unfold(stored):
    halfway = stored.shape[1] // BLOCK_TOKENS_N
    blocks = stored.reshape(2, halfway, BLOCK_TOKENS_N, stored.shape[2])
    return jnp.concatenate([blocks[0], blocks[1][::-1]], axis=0)


def refold(blocks):
    halfway = blocks.shape[0] // 2
    paired = jnp.stack([blocks[:halfway], blocks[halfway:][::-1]], axis=0)
    return paired.reshape(2, halfway * BLOCK_TOKENS_N, blocks.shape[2])


def live_entries(listed_blocks):
    same_block = listed_blocks[:, None] == listed_blocks[None, :]
    ordinal = jnp.arange(listed_blocks.shape[0], dtype=jnp.int32)
    earlier = ordinal[None, :] < ordinal[:, None]
    return jnp.logical_not(jnp.any(same_block & earlier, axis=1))


def allowed_mask(listed_blocks, live_entry, qblock):
    offsets = jnp.arange(BLOCK_TOKENS_N, dtype=jnp.int32)
    causal = offsets[None, :] <= offsets[:, None]
    diagonal = listed_blocks == qblock
    allowed = live_entry[:, None, None] & (jnp.logical_not(diagonal)[:, None, None] | causal[None])
    return jnp.transpose(allowed, (1, 0, 2)).reshape(BLOCK_TOKENS_N, KEY_LIST_SIZE * BLOCK_TOKENS_N)


def reference(queries, key_states, value_state_rows, grad_out, layouts, plant_ids):
    head_groups = QUERY_HEADS_N // KEY_VALUE_HEADS
    scaling = HEAD_SIZE ** -0.5
    query_blocks = unfold(queries)
    key_block_list = unfold(key_states)
    value_block_list = unfold(value_state_rows)
    grad_blocks = unfold(grad_out)
    count_of_blocks = query_blocks.shape[0]
    ordinal = jnp.arange(count_of_blocks, dtype=jnp.int32)
    listed_all = layouts[plant_ids, ordinal]

    def per_block(carry, inputs):
        key_accumulator, value_accumulator = carry
        qblock, query_row_values, gradient_rows, listed_blocks = inputs
        live_entry = live_entries(listed_blocks)
        allowed = allowed_mask(listed_blocks, live_entry, qblock)
        query_head_rows = query_row_values.astype(jnp.float32).reshape(BLOCK_TOKENS_N, KEY_VALUE_HEADS, head_groups, HEAD_SIZE)
        gradient_heads = gradient_rows.astype(jnp.float32).reshape(BLOCK_TOKENS_N, KEY_VALUE_HEADS, head_groups, HEAD_SIZE)
        key_head_rows = key_block_list[listed_blocks].astype(jnp.float32).reshape(KEY_LIST_SIZE * BLOCK_TOKENS_N, KEY_VALUE_HEADS, HEAD_SIZE)
        value_head_rows = value_block_list[listed_blocks].astype(jnp.float32).reshape(KEY_LIST_SIZE * BLOCK_TOKENS_N, KEY_VALUE_HEADS, HEAD_SIZE)
        scores = jnp.einsum('qhgd,khd->hgqk', query_head_rows, key_head_rows) * scaling
        scores = jnp.where(allowed[None, None], scores, -1e30)
        row_max = jnp.max(scores, axis=-1, keepdims=True)
        exponent = jnp.exp(scores - row_max)
        normed = exponent / jnp.sum(exponent, axis=-1, keepdims=True)
        weights = lax.optimization_barrier(normed.astype(jnp.bfloat16)).astype(jnp.float32)
        block_out = jnp.einsum('hgqk,khd->qhgd', weights, value_head_rows).astype(jnp.bfloat16).reshape(BLOCK_TOKENS_N, QUERY_HEADS_N * HEAD_SIZE)
        grad_probs = jnp.einsum('qhgd,khd->hgqk', gradient_heads, value_head_rows)
        row_delta = jnp.sum(normed * grad_probs, axis=-1, keepdims=True)
        grad_scores = lax.optimization_barrier((normed * (grad_probs - row_delta)).astype(jnp.bfloat16)).astype(jnp.float32)
        block_dq = (jnp.einsum('hgqk,khd->qhgd', grad_scores, key_head_rows) * scaling).astype(jnp.bfloat16).reshape(BLOCK_TOKENS_N, QUERY_HEADS_N * HEAD_SIZE)
        key_portion = jnp.einsum('hgqk,qhgd->khd', grad_scores, query_head_rows) * scaling
        value_portion = jnp.einsum('hgqk,qhgd->khd', weights, gradient_heads)
        keep_flags = live_entry.astype(jnp.float32)[:, None, None]
        key_accumulator = key_accumulator.at[listed_blocks].add(key_portion.reshape(KEY_LIST_SIZE, BLOCK_TOKENS_N, KEY_VALUE_HEADS * HEAD_SIZE) * keep_flags)
        value_accumulator = value_accumulator.at[listed_blocks].add(value_portion.reshape(KEY_LIST_SIZE, BLOCK_TOKENS_N, KEY_VALUE_HEADS * HEAD_SIZE) * keep_flags)
        return (key_accumulator, value_accumulator), (block_out, block_dq)

    zeros_key_value = jnp.zeros((count_of_blocks, BLOCK_TOKENS_N, KEY_VALUE_HEADS * HEAD_SIZE), jnp.float32)
    (key_accumulator, value_accumulator), (outputs, query_grads) = lax.scan(per_block, (zeros_key_value, zeros_key_value), (ordinal, query_blocks, grad_blocks, listed_all))
    return (refold(outputs), refold(query_grads), refold(key_accumulator.astype(jnp.bfloat16)), refold(value_accumulator.astype(jnp.bfloat16)))
```

```python
import jax
import jax.numpy as jnp
from jax import lax
from jax.sharding import PartitionSpec as P

HEAD_SIZE = 128
BLOCK_TOKENS_N = 64
KEY_LIST_SIZE = 8


def live_entries(listed_blocks):
    same_block = listed_blocks[:, None] == listed_blocks[None, :]
    ordinal = jnp.arange(listed_blocks.shape[0], dtype=jnp.int32)
    earlier = ordinal[None, :] < ordinal[:, None]
    return jnp.logical_not(jnp.any(same_block & earlier, axis=1))


def allowed_mask(listed_blocks, live_entry, qblock):
    offsets = jnp.arange(BLOCK_TOKENS_N, dtype=jnp.int32)
    causal = offsets[None, :] <= offsets[:, None]
    diagonal = listed_blocks == qblock
    allowed = live_entry[:, None, None] & (jnp.logical_not(diagonal)[:, None, None] | causal[None])
    return jnp.transpose(allowed, (1, 0, 2)).reshape(BLOCK_TOKENS_N, KEY_LIST_SIZE * BLOCK_TOKENS_N)


def attend_block(query_row_values, gradient_rows, keys_sel, values_sel, allowed, scaling):
    kv_heads = keys_sel.shape[2] // HEAD_SIZE
    head_groups = query_row_values.shape[1] // (kv_heads * HEAD_SIZE)
    query_head_rows = query_row_values.reshape(BLOCK_TOKENS_N, kv_heads, head_groups, HEAD_SIZE)
    gradient_heads = gradient_rows.reshape(BLOCK_TOKENS_N, kv_heads, head_groups, HEAD_SIZE)
    key_head_rows = keys_sel.reshape(KEY_LIST_SIZE * BLOCK_TOKENS_N, kv_heads, HEAD_SIZE)
    value_head_rows = values_sel.reshape(KEY_LIST_SIZE * BLOCK_TOKENS_N, kv_heads, HEAD_SIZE)
    scores = (
        jnp.einsum(
            "qhgd,khd->hgqk", query_head_rows, key_head_rows, preferred_element_type=jnp.float32
        )
        * scaling
    )
    scores = jnp.where(allowed[None, None], scores, -1e30)
    row_max = jnp.max(scores, axis=-1, keepdims=True)
    exponent = jnp.exp(scores - row_max)
    normed = exponent / jnp.sum(exponent, axis=-1, keepdims=True)
    weights = normed.astype(jnp.bfloat16)
    block_out = jnp.einsum(
        "hgqk,khd->qhgd", weights, value_head_rows, preferred_element_type=jnp.float32
    )
    block_out = block_out.astype(jnp.bfloat16).reshape(BLOCK_TOKENS_N, -1)
    grad_probs = jnp.einsum(
        "qhgd,khd->hgqk", gradient_heads, value_head_rows, preferred_element_type=jnp.float32
    )
    row_delta = jnp.sum(normed * grad_probs, axis=-1, keepdims=True)
    grad_scores = (normed * (grad_probs - row_delta)).astype(jnp.bfloat16)
    block_dq = (
        jnp.einsum("hgqk,khd->qhgd", grad_scores, key_head_rows, preferred_element_type=jnp.float32)
        * scaling
    )
    block_dq = block_dq.astype(jnp.bfloat16).reshape(BLOCK_TOKENS_N, -1)
    key_portion = (
        jnp.einsum(
            "hgqk,qhgd->khd", grad_scores, query_head_rows, preferred_element_type=jnp.float32
        )
        * scaling
    )
    value_portion = jnp.einsum(
        "hgqk,qhgd->khd", weights, gradient_heads, preferred_element_type=jnp.float32
    )
    key_portion = key_portion.reshape(KEY_LIST_SIZE, BLOCK_TOKENS_N, kv_heads * HEAD_SIZE)
    value_portion = value_portion.reshape(KEY_LIST_SIZE, BLOCK_TOKENS_N, kv_heads * HEAD_SIZE)
    return (block_out, block_dq, key_portion, value_portion)


def body(queries, key_states, value_state_rows, grad_out, layouts, plant_ids):
    scaling = HEAD_SIZE ** (-0.5)
    seq_count = lax.axis_size("seq")
    device = lax.axis_index("seq")
    count_of_blocks = layouts.shape[1]
    halfway = count_of_blocks // 2
    stacked = jnp.stack([key_states, value_state_rows])
    mine = lax.all_to_all(stacked, "head", split_axis=3, concat_axis=2, tiled=True)
    qblocks = jnp.stack([device, count_of_blocks - 1 - device])
    pick_block = jnp.arange(count_of_blocks, dtype=jnp.int32)[None, :] == qblocks[:, None]
    plant_of = jnp.sum(jnp.where(pick_block, plant_ids[None, :], 0), axis=1)
    pick_plant = jnp.arange(layouts.shape[0], dtype=jnp.int32)[None, :] == plant_of[:, None]
    picked = pick_plant[:, :, None, None] & pick_block[:, None, :, None]
    listed_all = jnp.sum(jnp.where(picked, layouts[None], 0), axis=(1, 2))
    owners = jnp.where(listed_all < halfway, listed_all, count_of_blocks - 1 - listed_all)
    upper_half = (listed_all >= halfway).astype(jnp.int32)
    slot_of = jnp.where(owners == device, seq_count + upper_half, owners)
    dest = jnp.arange(seq_count, dtype=jnp.int32)
    send_lower = (dest >= device)[:, None, None, None]
    send = jnp.where(send_lower, mine[:, 0][None], mine[:, 1][None])
    received = lax.all_to_all(send, "seq", split_axis=0, concat_axis=0, tiled=True)
    pool = jnp.concatenate(
        [received, jnp.stack([mine[:, 0], mine[:, 1]])], axis=0
    )
    width = mine.shape[3]
    key_buffer = jnp.zeros((seq_count + 2, BLOCK_TOKENS_N, width), jnp.float32)
    value_buffer = jnp.zeros((seq_count + 2, BLOCK_TOKENS_N, width), jnp.float32)
    slot_ids = jnp.arange(seq_count + 2, dtype=jnp.int32)
    outputs = []
    query_grads = []
    for which_half in range(2):
        listed_blocks = listed_all[which_half]
        live_entry = live_entries(listed_blocks)
        allowed = allowed_mask(listed_blocks, live_entry, qblocks[which_half])
        chosen = pool[slot_of[which_half]]
        block_out, block_dq, key_portion, value_portion = attend_block(
            queries[which_half],
            grad_out[which_half],
            chosen[:, 0],
            chosen[:, 1],
            allowed,
            scaling,
        )
        outputs.append(block_out)
        query_grads.append(block_dq)
        routing = (
            (slot_ids[:, None] == slot_of[which_half][None, :]) & live_entry[None, :]
        ).astype(jnp.float32)
        key_buffer = key_buffer + jnp.einsum(
            "sj,jbf->sbf", routing, key_portion, precision=lax.Precision.HIGHEST
        )
        value_buffer = value_buffer + jnp.einsum(
            "sj,jbf->sbf", routing, value_portion, precision=lax.Precision.HIGHEST
        )
    partials = jnp.stack([key_buffer[:seq_count], value_buffer[:seq_count]], axis=1)
    back = lax.all_to_all(
        partials.astype(jnp.bfloat16), "seq", split_axis=0, concat_axis=0, tiled=True
    ).astype(jnp.float32)
    source = jnp.arange(seq_count, dtype=jnp.int32)
    from_higher = (source > device).astype(jnp.float32)[:, None, None, None]
    from_lower = (source < device).astype(jnp.float32)[:, None, None, None]
    own = jnp.stack([key_buffer[seq_count:], value_buffer[seq_count:]])
    lower_total = own[:, 0] + jnp.sum(back * from_higher, axis=0)
    upper_total = own[:, 1] + jnp.sum(back * from_lower, axis=0)
    totals = jnp.stack([lower_total, upper_total], axis=1).astype(jnp.bfloat16)
    grads = lax.all_to_all(totals, "head", split_axis=2, concat_axis=3, tiled=True)
    return (jnp.stack(outputs), jnp.stack(query_grads), grads[0], grads[1])


def solution(mesh):
    in_specs = (
        P(None, "seq", "head"),
        P(None, ("seq", "head"), None),
        P(None, ("seq", "head"), None),
        P(None, "seq", "head"),
        P(),
        P(),
    )
    out_specs = (
        P(None, "seq", "head"),
        P(None, "seq", "head"),
        P(None, ("seq", "head"), None),
        P(None, ("seq", "head"), None),
    )
    return jax.shard_map(body, mesh=mesh, in_specs=in_specs, out_specs=out_specs, check_vma=False)
```

```python
import jax
import jax.numpy as jnp
from jax import lax
from jax.sharding import PartitionSpec as P
import functools
from jax.experimental import pallas as pl
from jax.experimental.pallas import tpu as pltpu

HEAD_SIZE = 128
BLOCK_TOKENS_N = 64
KEY_LIST_SIZE = 8


def live_entries(listed_blocks):
    same_block = listed_blocks[:, None] == listed_blocks[None, :]
    ordinal = jnp.arange(listed_blocks.shape[0], dtype=jnp.int32)
    earlier = ordinal[None, :] < ordinal[:, None]
    return jnp.logical_not(jnp.any(same_block & earlier, axis=1))


def allowed_mask(listed_blocks, live_entry, qblock):
    offsets = jnp.arange(BLOCK_TOKENS_N, dtype=jnp.int32)
    causal = offsets[None, :] <= offsets[:, None]
    diagonal = listed_blocks == qblock
    allowed = live_entry[:, None, None] & (jnp.logical_not(diagonal)[:, None, None] | causal[None])
    return jnp.transpose(allowed, (1, 0, 2)).reshape(BLOCK_TOKENS_N, KEY_LIST_SIZE * BLOCK_TOKENS_N)


def attention_kernel(meta_ref, q_ref, do_ref, recv_ref, mine_ref,
                     out_ref, dq_ref, send_ref, own_ref, acc_ref, *, scaling):
    seq_count = recv_ref.shape[0]
    groups = q_ref.shape[2] // HEAD_SIZE
    rows = groups * BLOCK_TOKENS_N
    cols = KEY_LIST_SIZE * BLOCK_TOKENS_N
    acc_ref[...] = jnp.zeros_like(acc_ref)
    col = lax.broadcasted_iota(jnp.int32, (1, cols), 1)
    col_block = col // BLOCK_TOKENS_N
    key_pos = col % BLOCK_TOKENS_N
    query_pos = lax.broadcasted_iota(jnp.int32, (rows, 1), 0) % BLOCK_TOKENS_N
    for half in range(2):
        keys, values = [], []
        live_row = jnp.zeros((1, cols), jnp.int32)
        diag_row = jnp.zeros((1, cols), jnp.int32)
        for j in range(KEY_LIST_SIZE):
            slot = meta_ref[half, 0, j]
            from_recv = slot < seq_count
            r = jnp.minimum(slot, seq_count - 1)
            m = jnp.maximum(slot - seq_count, 0)
            keys.append(jnp.where(from_recv, recv_ref[r, 0], mine_ref[0, m]))
            values.append(jnp.where(from_recv, recv_ref[r, 1], mine_ref[1, m]))
            live_row = jnp.where(col_block == j, meta_ref[half, 1, j], live_row)
            diag_row = jnp.where(col_block == j, meta_ref[half, 2, j], diag_row)
        key_all = jnp.concatenate(keys, axis=0)
        value_all = jnp.concatenate(values, axis=0)
        query_all = jnp.concatenate(
            [q_ref[half, :, g * HEAD_SIZE:(g + 1) * HEAD_SIZE] for g in range(groups)], axis=0)
        grad_all = jnp.concatenate(
            [do_ref[half, :, g * HEAD_SIZE:(g + 1) * HEAD_SIZE] for g in range(groups)], axis=0)
        allowed = (live_row != 0) & ((diag_row == 0) | (key_pos <= query_pos))
        nt = (((1,), (1,)), ((), ()))
        tn = (((0,), (0,)), ((), ()))
        scores = lax.dot_general(query_all, key_all, nt, preferred_element_type=jnp.float32) * scaling
        scores = jnp.where(allowed, scores, -1e30)
        row_max = jnp.max(scores, axis=1, keepdims=True)
        exponent = jnp.exp(scores - row_max)
        normed = exponent / jnp.sum(exponent, axis=1, keepdims=True)
        weights = normed.astype(jnp.bfloat16)
        block_out = jnp.dot(weights, value_all, preferred_element_type=jnp.float32).astype(out_ref.dtype)
        grad_probs = lax.dot_general(grad_all, value_all, nt, preferred_element_type=jnp.float32)
        row_delta = jnp.sum(normed * grad_probs, axis=1, keepdims=True)
        grad_scores = (normed * (grad_probs - row_delta)).astype(jnp.bfloat16)
        block_dq = (jnp.dot(grad_scores, key_all, preferred_element_type=jnp.float32) * scaling).astype(dq_ref.dtype)
        for g in range(groups):
            out_ref[half, :, g * HEAD_SIZE:(g + 1) * HEAD_SIZE] = block_out[g * BLOCK_TOKENS_N:(g + 1) * BLOCK_TOKENS_N]
            dq_ref[half, :, g * HEAD_SIZE:(g + 1) * HEAD_SIZE] = block_dq[g * BLOCK_TOKENS_N:(g + 1) * BLOCK_TOKENS_N]
        key_portion = lax.dot_general(grad_scores, query_all, tn, preferred_element_type=jnp.float32) * scaling
        value_portion = lax.dot_general(weights, grad_all, tn, preferred_element_type=jnp.float32)
        for j in range(KEY_LIST_SIZE):
            slot = meta_ref[half, 0, j]
            keep = meta_ref[half, 1, j] != 0
            piece = slice(j * BLOCK_TOKENS_N, (j + 1) * BLOCK_TOKENS_N)
            acc_ref[slot, 0] += jnp.where(keep, key_portion[piece], 0.0)
            acc_ref[slot, 1] += jnp.where(keep, value_portion[piece], 0.0)
    send_ref[...] = acc_ref[:seq_count].astype(send_ref.dtype)
    own_ref[...] = acc_ref[seq_count:]


def attention_call(meta, queries, grad_out, received, mine, scaling):
    seq_count = received.shape[0]
    width = received.shape[3]
    vmem = pltpu.VMEM
    smem = pltpu.SMEM
    return pl.pallas_call(
        functools.partial(attention_kernel, scaling=scaling),
        out_shape=(
            jax.ShapeDtypeStruct(queries.shape, queries.dtype),
            jax.ShapeDtypeStruct(queries.shape, queries.dtype),
            jax.ShapeDtypeStruct(received.shape, received.dtype),
            jax.ShapeDtypeStruct((2, 2, BLOCK_TOKENS_N, width), jnp.float32),
        ),
        in_specs=[pl.BlockSpec(memory_space=smem)] + [pl.BlockSpec(memory_space=vmem)] * 4,
        out_specs=[pl.BlockSpec(memory_space=vmem)] * 4,
        scratch_shapes=[pltpu.VMEM((seq_count + 2, 2, BLOCK_TOKENS_N, width), jnp.float32)],
        compiler_params=pltpu.CompilerParams(vmem_limit_bytes=48 * 1024 * 1024),
    )(meta, queries, grad_out, received, mine)


def body(queries, key_states, value_state_rows, grad_out, layouts, plant_ids):
    scaling = HEAD_SIZE ** (-0.5)
    seq_count = lax.axis_size("seq")
    device = lax.axis_index("seq")
    count_of_blocks = layouts.shape[1]
    halfway = count_of_blocks // 2
    stacked = jnp.stack([key_states, value_state_rows])
    mine = lax.all_to_all(stacked, "head", split_axis=3, concat_axis=2, tiled=True)
    qblocks = jnp.stack([device, count_of_blocks - 1 - device])
    pick_block = jnp.arange(count_of_blocks, dtype=jnp.int32)[None, :] == qblocks[:, None]
    plant_of = jnp.sum(jnp.where(pick_block, plant_ids[None, :], 0), axis=1)
    pick_plant = jnp.arange(layouts.shape[0], dtype=jnp.int32)[None, :] == plant_of[:, None]
    picked = pick_plant[:, :, None, None] & pick_block[:, None, :, None]
    listed_all = jnp.sum(jnp.where(picked, layouts[None], 0), axis=(1, 2))
    owners = jnp.where(listed_all < halfway, listed_all, count_of_blocks - 1 - listed_all)
    upper_half = (listed_all >= halfway).astype(jnp.int32)
    slot_of = jnp.where(owners == device, seq_count + upper_half, owners)
    live = jnp.stack([live_entries(listed_all[h]) for h in range(2)]).astype(jnp.int32)
    diagonal = (listed_all == qblocks[:, None]).astype(jnp.int32)
    meta = jnp.stack([slot_of, live, diagonal], axis=1)
    dest = jnp.arange(seq_count, dtype=jnp.int32)
    send_lower = (dest >= device)[:, None, None, None]
    send = jnp.where(send_lower, mine[:, 0][None], mine[:, 1][None])
    received = lax.all_to_all(send, "seq", split_axis=0, concat_axis=0, tiled=True)
    outputs, query_grads, partials, own = attention_call(
        meta, queries, grad_out, received, mine, scaling
    )
    back = lax.all_to_all(partials, "seq", split_axis=0, concat_axis=0, tiled=True).astype(
        jnp.float32
    )
    source = jnp.arange(seq_count, dtype=jnp.int32)
    from_higher = (source > device).astype(jnp.float32)[:, None, None, None]
    from_lower = (source < device).astype(jnp.float32)[:, None, None, None]
    lower_total = own[0] + jnp.sum(back * from_higher, axis=0)
    upper_total = own[1] + jnp.sum(back * from_lower, axis=0)
    totals = jnp.stack([lower_total, upper_total], axis=1).astype(jnp.bfloat16)
    grads = lax.all_to_all(totals, "head", split_axis=2, concat_axis=3, tiled=True)
    return (outputs, query_grads, grads[0], grads[1])


def solution(mesh):
    in_specs = (
        P(None, "seq", "head"),
        P(None, ("seq", "head"), None),
        P(None, ("seq", "head"), None),
        P(None, "seq", "head"),
        P(),
        P(),
    )
    out_specs = (
        P(None, "seq", "head"),
        P(None, "seq", "head"),
        P(None, ("seq", "head"), None),
        P(None, ("seq", "head"), None),
    )
    return jax.shard_map(body, mesh=mesh, in_specs=in_specs, out_specs=out_specs, check_vma=False)
```

```python
import jax
import jax.numpy as jnp
from jax import lax
from jax.sharding import PartitionSpec as P
import functools
from jax.experimental import pallas as pl
from jax.experimental.pallas import tpu as pltpu

HEAD_SIZE = 128
BLOCK_TOKENS_N = 64
KEY_LIST_SIZE = 8


def live_entries(listed_blocks):
    same_block = listed_blocks[:, None] == listed_blocks[None, :]
    ordinal = jnp.arange(listed_blocks.shape[0], dtype=jnp.int32)
    earlier = ordinal[None, :] < ordinal[:, None]
    return jnp.logical_not(jnp.any(same_block & earlier, axis=1))


def allowed_mask(listed_blocks, live_entry, qblock):
    offsets = jnp.arange(BLOCK_TOKENS_N, dtype=jnp.int32)
    causal = offsets[None, :] <= offsets[:, None]
    diagonal = listed_blocks == qblock
    allowed = live_entry[:, None, None] & (jnp.logical_not(diagonal)[:, None, None] | causal[None])
    return jnp.transpose(allowed, (1, 0, 2)).reshape(BLOCK_TOKENS_N, KEY_LIST_SIZE * BLOCK_TOKENS_N)


def attention_kernel(meta_ref, q_ref, do_ref, recv_ref, mine_ref,
                     out_ref, dq_ref, send_ref, own_ref, acc_ref, *, scaling):
    seq_count = recv_ref.shape[0]
    groups = q_ref.shape[2] // HEAD_SIZE
    rows = groups * BLOCK_TOKENS_N
    cols = KEY_LIST_SIZE * BLOCK_TOKENS_N
    acc_ref[...] = jnp.zeros_like(acc_ref)
    col = lax.broadcasted_iota(jnp.int32, (1, cols), 1)
    col_block = col // BLOCK_TOKENS_N
    key_pos = col % BLOCK_TOKENS_N
    query_pos = lax.broadcasted_iota(jnp.int32, (rows, 1), 0) % BLOCK_TOKENS_N
    for half in range(2):
        keys, values = [], []
        live_row = jnp.zeros((1, cols), jnp.int32)
        diag_row = jnp.zeros((1, cols), jnp.int32)
        for j in range(KEY_LIST_SIZE):
            slot = meta_ref[half, 0, j]
            from_recv = slot < seq_count
            r = jnp.minimum(slot, seq_count - 1)
            m = jnp.maximum(slot - seq_count, 0)
            keys.append(jnp.where(from_recv, recv_ref[r, 0], mine_ref[0, m]))
            values.append(jnp.where(from_recv, recv_ref[r, 1], mine_ref[1, m]))
            live_row = jnp.where(col_block == j, meta_ref[half, 1, j], live_row)
            diag_row = jnp.where(col_block == j, meta_ref[half, 2, j], diag_row)
        key_all = jnp.concatenate(keys, axis=0)
        value_all = jnp.concatenate(values, axis=0)
        query_all = jnp.concatenate(
            [q_ref[half, :, g * HEAD_SIZE:(g + 1) * HEAD_SIZE] for g in range(groups)], axis=0)
        grad_all = jnp.concatenate(
            [do_ref[half, :, g * HEAD_SIZE:(g + 1) * HEAD_SIZE] for g in range(groups)], axis=0)
        allowed = (live_row != 0) & ((diag_row == 0) | (key_pos <= query_pos))
        nt = (((1,), (1,)), ((), ()))
        tn = (((0,), (0,)), ((), ()))
        scores = lax.dot_general(query_all, key_all, nt, preferred_element_type=jnp.float32) * scaling
        scores = jnp.where(allowed, scores, -1e30)
        row_max = jnp.max(scores, axis=1, keepdims=True)
        exponent = jnp.exp(scores - row_max)
        normed = exponent / jnp.sum(exponent, axis=1, keepdims=True)
        weights = normed.astype(jnp.bfloat16)
        block_out = jnp.dot(weights, value_all, preferred_element_type=jnp.float32).astype(out_ref.dtype)
        grad_probs = lax.dot_general(grad_all, value_all, nt, preferred_element_type=jnp.float32)
        row_delta = jnp.sum(normed * grad_probs, axis=1, keepdims=True)
        grad_scores = (normed * (grad_probs - row_delta)).astype(jnp.bfloat16)
        block_dq = (jnp.dot(grad_scores, key_all, preferred_element_type=jnp.float32) * scaling).astype(dq_ref.dtype)
        for g in range(groups):
            out_ref[half, :, g * HEAD_SIZE:(g + 1) * HEAD_SIZE] = block_out[g * BLOCK_TOKENS_N:(g + 1) * BLOCK_TOKENS_N]
            dq_ref[half, :, g * HEAD_SIZE:(g + 1) * HEAD_SIZE] = block_dq[g * BLOCK_TOKENS_N:(g + 1) * BLOCK_TOKENS_N]
        key_portion = lax.dot_general(grad_scores, query_all, tn, preferred_element_type=jnp.float32) * scaling
        value_portion = lax.dot_general(weights, grad_all, tn, preferred_element_type=jnp.float32)
        for j in range(KEY_LIST_SIZE):
            slot = meta_ref[half, 0, j]
            keep = meta_ref[half, 1, j] != 0
            piece = slice(j * BLOCK_TOKENS_N, (j + 1) * BLOCK_TOKENS_N)
            acc_ref[slot, 0] += jnp.where(keep, key_portion[piece], 0.0)
            acc_ref[slot, 1] += jnp.where(keep, value_portion[piece], 0.0)
    send_ref[...] = acc_ref[:seq_count].astype(send_ref.dtype)
    own_ref[...] = acc_ref[seq_count:]


def attention_call(meta, queries, grad_out, received, mine, scaling):
    seq_count = received.shape[0]
    width = received.shape[3]
    vmem = pltpu.VMEM
    smem = pltpu.SMEM
    return pl.pallas_call(
        functools.partial(attention_kernel, scaling=scaling),
        out_shape=(
            jax.ShapeDtypeStruct(queries.shape, queries.dtype),
            jax.ShapeDtypeStruct(queries.shape, queries.dtype),
            jax.ShapeDtypeStruct(received.shape, received.dtype),
            jax.ShapeDtypeStruct((2, 2, BLOCK_TOKENS_N, width), jnp.float32),
        ),
        in_specs=[pl.BlockSpec(memory_space=smem)] + [pl.BlockSpec(memory_space=vmem)] * 4,
        out_specs=[pl.BlockSpec(memory_space=vmem)] * 4,
        scratch_shapes=[pltpu.VMEM((seq_count + 2, 2, BLOCK_TOKENS_N, width), jnp.float32)],
        compiler_params=pltpu.CompilerParams(vmem_limit_bytes=48 * 1024 * 1024),
    )(meta, queries, grad_out, received, mine)


def body(queries, key_states, value_state_rows, grad_out, layouts, plant_ids):
    scaling = HEAD_SIZE ** (-0.5)
    seq_count = lax.axis_size("seq")
    device = lax.axis_index("seq")
    count_of_blocks = layouts.shape[1]
    halfway = count_of_blocks // 2
    head_count = lax.axis_size("head")
    rows = key_states.shape[1]
    width = key_states.shape[2] // head_count
    stacked = jnp.stack([key_states, value_state_rows]).reshape(2, 2, rows, head_count, width)
    outgoing = jnp.transpose(stacked, (3, 0, 1, 2, 4))
    incoming = lax.all_to_all(outgoing, "head", split_axis=0, concat_axis=0, tiled=True)
    mine = jnp.transpose(incoming, (1, 2, 0, 3, 4)).reshape(2, 2, head_count * rows, width)
    qblocks = jnp.stack([device, count_of_blocks - 1 - device])
    pick_block = jnp.arange(count_of_blocks, dtype=jnp.int32)[None, :] == qblocks[:, None]
    plant_of = jnp.sum(jnp.where(pick_block, plant_ids[None, :], 0), axis=1)
    pick_plant = jnp.arange(layouts.shape[0], dtype=jnp.int32)[None, :] == plant_of[:, None]
    picked = pick_plant[:, :, None, None] & pick_block[:, None, :, None]
    listed_all = jnp.sum(jnp.where(picked, layouts[None], 0), axis=(1, 2))
    owners = jnp.where(listed_all < halfway, listed_all, count_of_blocks - 1 - listed_all)
    upper_half = (listed_all >= halfway).astype(jnp.int32)
    slot_of = jnp.where(owners == device, seq_count + upper_half, owners)
    live = jnp.stack([live_entries(listed_all[h]) for h in range(2)]).astype(jnp.int32)
    diagonal = (listed_all == qblocks[:, None]).astype(jnp.int32)
    meta = jnp.stack([slot_of, live, diagonal], axis=1)
    dest = jnp.arange(seq_count, dtype=jnp.int32)
    send_lower = (dest >= device)[:, None, None, None]
    send = jnp.where(send_lower, mine[:, 0][None], mine[:, 1][None])
    received = lax.all_to_all(send, "seq", split_axis=0, concat_axis=0, tiled=True)
    outputs, query_grads, partials, own = attention_call(
        meta, queries, grad_out, received, mine, scaling
    )
    back = lax.all_to_all(partials, "seq", split_axis=0, concat_axis=0, tiled=True).astype(
        jnp.float32
    )
    source = jnp.arange(seq_count, dtype=jnp.int32)
    from_higher = (source > device).astype(jnp.float32)[:, None, None, None]
    from_lower = (source < device).astype(jnp.float32)[:, None, None, None]
    lower_total = own[0] + jnp.sum(back * from_higher, axis=0)
    upper_total = own[1] + jnp.sum(back * from_lower, axis=0)
    totals = jnp.stack([lower_total, upper_total], axis=1).astype(jnp.bfloat16)
    outgoing = jnp.transpose(totals.reshape(2, 2, head_count, rows, width), (2, 0, 1, 3, 4))
    incoming = lax.all_to_all(outgoing, "head", split_axis=0, concat_axis=0, tiled=True)
    grads = jnp.transpose(incoming, (1, 2, 3, 0, 4)).reshape(2, 2, rows, head_count * width)
    return (outputs, query_grads, grads[0], grads[1])


def solution(mesh):
    in_specs = (
        P(None, "seq", "head"),
        P(None, ("seq", "head"), None),
        P(None, ("seq", "head"), None),
        P(None, "seq", "head"),
        P(),
        P(),
    )
    out_specs = (
        P(None, "seq", "head"),
        P(None, "seq", "head"),
        P(None, ("seq", "head"), None),
        P(None, ("seq", "head"), None),
    )
    return jax.shard_map(body, mesh=mesh, in_specs=in_specs, out_specs=out_specs, check_vma=False)
```

```python
import jax
import jax.numpy as jnp
from jax import lax
from jax.sharding import PartitionSpec as P
import functools
from jax.experimental import pallas as pl
from jax.experimental.pallas import tpu as pltpu

HEAD_SIZE = 128
BLOCK_TOKENS_N = 64
KEY_LIST_SIZE = 8


def live_entries(listed_blocks):
    same_block = listed_blocks[:, None] == listed_blocks[None, :]
    ordinal = jnp.arange(listed_blocks.shape[0], dtype=jnp.int32)
    earlier = ordinal[None, :] < ordinal[:, None]
    return jnp.logical_not(jnp.any(same_block & earlier, axis=1))


def allowed_mask(listed_blocks, live_entry, qblock):
    offsets = jnp.arange(BLOCK_TOKENS_N, dtype=jnp.int32)
    causal = offsets[None, :] <= offsets[:, None]
    diagonal = listed_blocks == qblock
    allowed = live_entry[:, None, None] & (jnp.logical_not(diagonal)[:, None, None] | causal[None])
    return jnp.transpose(allowed, (1, 0, 2)).reshape(BLOCK_TOKENS_N, KEY_LIST_SIZE * BLOCK_TOKENS_N)


def attention_kernel(meta_ref, q_ref, do_ref, recv_ref, mine_ref,
                     out_ref, dq_ref, send_hbm, own_ref, acc_ref, send_ref, sem, *, scaling):
    seq_count = recv_ref.shape[0]
    groups = q_ref.shape[2] // HEAD_SIZE
    rows = groups * BLOCK_TOKENS_N
    cols = KEY_LIST_SIZE * BLOCK_TOKENS_N
    for half in range(2):
        for j in range(KEY_LIST_SIZE):
            acc_ref[meta_ref[half, 0, j]] = jnp.zeros(acc_ref.shape[1:], acc_ref.dtype)
    acc_ref[seq_count] = jnp.zeros(acc_ref.shape[1:], acc_ref.dtype)
    acc_ref[seq_count + 1] = jnp.zeros(acc_ref.shape[1:], acc_ref.dtype)
    send_ref[...] = jnp.zeros_like(send_ref)
    col = lax.broadcasted_iota(jnp.int32, (1, cols), 1)
    col_block = col // BLOCK_TOKENS_N
    key_pos = col % BLOCK_TOKENS_N
    query_pos = lax.broadcasted_iota(jnp.int32, (rows, 1), 0) % BLOCK_TOKENS_N
    for half in range(2):
        keys, values = [], []
        live_row = jnp.zeros((1, cols), jnp.int32)
        diag_row = jnp.zeros((1, cols), jnp.int32)
        for j in range(KEY_LIST_SIZE):
            slot = meta_ref[half, 0, j]
            from_recv = slot < seq_count
            r = jnp.minimum(slot, seq_count - 1)
            m = jnp.maximum(slot - seq_count, 0)
            keys.append(jnp.where(from_recv, recv_ref[r, 0], mine_ref[0, m]))
            values.append(jnp.where(from_recv, recv_ref[r, 1], mine_ref[1, m]))
            live_row = jnp.where(col_block == j, meta_ref[half, 1, j], live_row)
            diag_row = jnp.where(col_block == j, meta_ref[half, 2, j], diag_row)
        key_all = jnp.concatenate(keys, axis=0)
        value_all = jnp.concatenate(values, axis=0)
        query_all = jnp.concatenate(
            [q_ref[half, :, g * HEAD_SIZE:(g + 1) * HEAD_SIZE] for g in range(groups)], axis=0)
        grad_all = jnp.concatenate(
            [do_ref[half, :, g * HEAD_SIZE:(g + 1) * HEAD_SIZE] for g in range(groups)], axis=0)
        allowed = (live_row != 0) & ((diag_row == 0) | (key_pos <= query_pos))
        nt = (((1,), (1,)), ((), ()))
        tn = (((0,), (0,)), ((), ()))
        scores = lax.dot_general(query_all, key_all, nt, preferred_element_type=jnp.float32) * scaling
        scores = jnp.where(allowed, scores, -1e30)
        row_max = jnp.max(scores, axis=1, keepdims=True)
        exponent = jnp.exp(scores - row_max)
        normed = exponent / jnp.sum(exponent, axis=1, keepdims=True)
        weights = normed.astype(jnp.bfloat16)
        block_out = jnp.dot(weights, value_all, preferred_element_type=jnp.float32).astype(out_ref.dtype)
        grad_probs = lax.dot_general(grad_all, value_all, nt, preferred_element_type=jnp.float32)
        row_delta = jnp.sum(normed * grad_probs, axis=1, keepdims=True)
        grad_scores = (normed * (grad_probs - row_delta)).astype(jnp.bfloat16)
        block_dq = (jnp.dot(grad_scores, key_all, preferred_element_type=jnp.float32) * scaling).astype(dq_ref.dtype)
        for g in range(groups):
            out_ref[half, :, g * HEAD_SIZE:(g + 1) * HEAD_SIZE] = block_out[g * BLOCK_TOKENS_N:(g + 1) * BLOCK_TOKENS_N]
            dq_ref[half, :, g * HEAD_SIZE:(g + 1) * HEAD_SIZE] = block_dq[g * BLOCK_TOKENS_N:(g + 1) * BLOCK_TOKENS_N]
        key_portion = lax.dot_general(grad_scores, query_all, tn, preferred_element_type=jnp.float32) * scaling
        value_portion = lax.dot_general(weights, grad_all, tn, preferred_element_type=jnp.float32)
        for j in range(KEY_LIST_SIZE):
            slot = meta_ref[half, 0, j]
            keep = meta_ref[half, 1, j] != 0
            piece = slice(j * BLOCK_TOKENS_N, (j + 1) * BLOCK_TOKENS_N)
            acc_ref[slot, 0] += jnp.where(keep, key_portion[piece], 0.0)
            acc_ref[slot, 1] += jnp.where(keep, value_portion[piece], 0.0)
    for half in range(2):
        for j in range(KEY_LIST_SIZE):
            slot = meta_ref[half, 0, j]
            r = jnp.minimum(slot, seq_count - 1)

            @pl.when(slot < seq_count)
            def _():
                send_ref[r] = acc_ref[r].astype(send_ref.dtype)

    copy = pltpu.make_async_copy(send_ref, send_hbm, sem)
    copy.start()
    own_ref[...] = acc_ref[seq_count:]
    copy.wait()


def attention_call(meta, queries, grad_out, received, mine, scaling):
    seq_count = received.shape[0]
    width = received.shape[3]
    vmem = pltpu.VMEM
    smem = pltpu.SMEM
    return pl.pallas_call(
        functools.partial(attention_kernel, scaling=scaling),
        out_shape=(
            jax.ShapeDtypeStruct(queries.shape, queries.dtype),
            jax.ShapeDtypeStruct(queries.shape, queries.dtype),
            jax.ShapeDtypeStruct(received.shape, received.dtype),
            jax.ShapeDtypeStruct((2, 2, BLOCK_TOKENS_N, width), jnp.float32),
        ),
        in_specs=[pl.BlockSpec(memory_space=smem)] + [pl.BlockSpec(memory_space=vmem)] * 4,
        out_specs=[
            pl.BlockSpec(memory_space=vmem),
            pl.BlockSpec(memory_space=vmem),
            pl.BlockSpec(memory_space=pl.ANY),
            pl.BlockSpec(memory_space=vmem),
        ],
        scratch_shapes=[
            pltpu.VMEM((seq_count + 2, 2, BLOCK_TOKENS_N, width), jnp.float32),
            pltpu.VMEM(received.shape, received.dtype),
            pltpu.SemaphoreType.DMA(()),
        ],
        compiler_params=pltpu.CompilerParams(vmem_limit_bytes=48 * 1024 * 1024),
    )(meta, queries, grad_out, received, mine)


def body(queries, key_states, value_state_rows, grad_out, layouts, plant_ids):
    scaling = HEAD_SIZE ** (-0.5)
    seq_count = lax.axis_size("seq")
    device = lax.axis_index("seq")
    count_of_blocks = layouts.shape[1]
    halfway = count_of_blocks // 2
    head_count = lax.axis_size("head")
    rows = key_states.shape[1]
    width = key_states.shape[2] // head_count
    stacked = jnp.stack([key_states, value_state_rows]).reshape(2, 2, rows, head_count, width)
    outgoing = jnp.transpose(stacked, (3, 0, 1, 2, 4))
    incoming = lax.all_to_all(outgoing, "head", split_axis=0, concat_axis=0, tiled=True)
    mine = jnp.transpose(incoming, (1, 2, 0, 3, 4)).reshape(2, 2, head_count * rows, width)
    qblocks = jnp.stack([device, count_of_blocks - 1 - device])
    pick_block = jnp.arange(count_of_blocks, dtype=jnp.int32)[None, :] == qblocks[:, None]
    plant_of = jnp.sum(jnp.where(pick_block, plant_ids[None, :], 0), axis=1)
    pick_plant = jnp.arange(layouts.shape[0], dtype=jnp.int32)[None, :] == plant_of[:, None]
    picked = pick_plant[:, :, None, None] & pick_block[:, None, :, None]
    listed_all = jnp.sum(jnp.where(picked, layouts[None], 0), axis=(1, 2))
    owners = jnp.where(listed_all < halfway, listed_all, count_of_blocks - 1 - listed_all)
    upper_half = (listed_all >= halfway).astype(jnp.int32)
    slot_of = jnp.where(owners == device, seq_count + upper_half, owners)
    live = jnp.stack([live_entries(listed_all[h]) for h in range(2)]).astype(jnp.int32)
    diagonal = (listed_all == qblocks[:, None]).astype(jnp.int32)
    meta = jnp.stack([slot_of, live, diagonal], axis=1)
    dest = jnp.arange(seq_count, dtype=jnp.int32)
    send_lower = (dest >= device)[:, None, None, None]
    send = jnp.where(send_lower, mine[:, 0][None], mine[:, 1][None])
    received = lax.all_to_all(send, "seq", split_axis=0, concat_axis=0, tiled=True)
    outputs, query_grads, partials, own = attention_call(
        meta, queries, grad_out, received, mine, scaling
    )
    back = lax.all_to_all(partials, "seq", split_axis=0, concat_axis=0, tiled=True).astype(
        jnp.float32
    )
    source = jnp.arange(seq_count, dtype=jnp.int32)
    from_higher = (source > device).astype(jnp.float32)[:, None, None, None]
    from_lower = (source < device).astype(jnp.float32)[:, None, None, None]
    lower_total = own[0] + jnp.sum(back * from_higher, axis=0)
    upper_total = own[1] + jnp.sum(back * from_lower, axis=0)
    totals = jnp.stack([lower_total, upper_total], axis=1).astype(jnp.bfloat16)
    outgoing = jnp.transpose(totals.reshape(2, 2, head_count, rows, width), (2, 0, 1, 3, 4))
    incoming = lax.all_to_all(outgoing, "head", split_axis=0, concat_axis=0, tiled=True)
    grads = jnp.transpose(incoming, (1, 2, 3, 0, 4)).reshape(2, 2, rows, head_count * width)
    return (outputs, query_grads, grads[0], grads[1])


def solution(mesh):
    in_specs = (
        P(None, "seq", "head"),
        P(None, ("seq", "head"), None),
        P(None, ("seq", "head"), None),
        P(None, "seq", "head"),
        P(),
        P(),
    )
    out_specs = (
        P(None, "seq", "head"),
        P(None, "seq", "head"),
        P(None, ("seq", "head"), None),
        P(None, ("seq", "head"), None),
    )
    return jax.shard_map(body, mesh=mesh, in_specs=in_specs, out_specs=out_specs, check_vma=False)
```

```python
import jax
import jax.numpy as jnp
from jax import lax
from jax.sharding import PartitionSpec as P
import functools
from jax.experimental import pallas as pl
from jax.experimental.pallas import tpu as pltpu

HEAD_SIZE = 128
BLOCK_TOKENS_N = 64
KEY_LIST_SIZE = 8


def live_entries(listed_blocks):
    same_block = listed_blocks[:, None] == listed_blocks[None, :]
    ordinal = jnp.arange(listed_blocks.shape[0], dtype=jnp.int32)
    earlier = ordinal[None, :] < ordinal[:, None]
    return jnp.logical_not(jnp.any(same_block & earlier, axis=1))


def allowed_mask(listed_blocks, live_entry, qblock):
    offsets = jnp.arange(BLOCK_TOKENS_N, dtype=jnp.int32)
    causal = offsets[None, :] <= offsets[:, None]
    diagonal = listed_blocks == qblock
    allowed = live_entry[:, None, None] & (jnp.logical_not(diagonal)[:, None, None] | causal[None])
    return jnp.transpose(allowed, (1, 0, 2)).reshape(BLOCK_TOKENS_N, KEY_LIST_SIZE * BLOCK_TOKENS_N)


def attention_kernel(meta_ref, q_ref, do_ref, recv_ref, mine_ref,
                     out_ref, dq_ref, send_ref, own_ref, acc_ref, *, scaling):
    seq_count = recv_ref.shape[0]
    groups = q_ref.shape[2] // HEAD_SIZE
    rows = groups * BLOCK_TOKENS_N
    cols = KEY_LIST_SIZE * BLOCK_TOKENS_N
    for half in range(2):
        for j in range(KEY_LIST_SIZE):
            acc_ref[meta_ref[half, 0, j]] = jnp.zeros(acc_ref.shape[1:], acc_ref.dtype)
    col = lax.broadcasted_iota(jnp.int32, (1, cols), 1)
    col_block = col // BLOCK_TOKENS_N
    key_pos = col % BLOCK_TOKENS_N
    query_pos = lax.broadcasted_iota(jnp.int32, (rows, 1), 0) % BLOCK_TOKENS_N
    for half in range(2):
        keys, values = [], []
        live_row = jnp.zeros((1, cols), jnp.int32)
        diag_row = jnp.zeros((1, cols), jnp.int32)
        for j in range(KEY_LIST_SIZE):
            slot = meta_ref[half, 0, j]
            from_recv = slot < seq_count
            r = jnp.minimum(slot, seq_count - 1)
            m = jnp.maximum(slot - seq_count, 0)
            keys.append(jnp.where(from_recv, recv_ref[r, 0], mine_ref[0, m]))
            values.append(jnp.where(from_recv, recv_ref[r, 1], mine_ref[1, m]))
            live_row = jnp.where(col_block == j, meta_ref[half, 1, j], live_row)
            diag_row = jnp.where(col_block == j, meta_ref[half, 2, j], diag_row)
        key_all = jnp.concatenate(keys, axis=0)
        value_all = jnp.concatenate(values, axis=0)
        query_all = jnp.concatenate(
            [q_ref[half, :, g * HEAD_SIZE:(g + 1) * HEAD_SIZE] for g in range(groups)], axis=0)
        grad_all = jnp.concatenate(
            [do_ref[half, :, g * HEAD_SIZE:(g + 1) * HEAD_SIZE] for g in range(groups)], axis=0)
        allowed = (live_row != 0) & ((diag_row == 0) | (key_pos <= query_pos))
        nt = (((1,), (1,)), ((), ()))
        tn = (((0,), (0,)), ((), ()))
        scores = lax.dot_general(query_all, key_all, nt, preferred_element_type=jnp.float32) * scaling
        scores = jnp.where(allowed, scores, -1e30)
        row_max = jnp.max(scores, axis=1, keepdims=True)
        exponent = jnp.exp(scores - row_max)
        normed = exponent / jnp.sum(exponent, axis=1, keepdims=True)
        weights = normed.astype(jnp.bfloat16)
        block_out = jnp.dot(weights, value_all, preferred_element_type=jnp.float32).astype(out_ref.dtype)
        grad_probs = lax.dot_general(grad_all, value_all, nt, preferred_element_type=jnp.float32)
        row_delta = jnp.sum(normed * grad_probs, axis=1, keepdims=True)
        grad_scores = (normed * (grad_probs - row_delta)).astype(jnp.bfloat16)
        block_dq = (jnp.dot(grad_scores, key_all, preferred_element_type=jnp.float32) * scaling).astype(dq_ref.dtype)
        for g in range(groups):
            out_ref[half, :, g * HEAD_SIZE:(g + 1) * HEAD_SIZE] = block_out[g * BLOCK_TOKENS_N:(g + 1) * BLOCK_TOKENS_N]
            dq_ref[half, :, g * HEAD_SIZE:(g + 1) * HEAD_SIZE] = block_dq[g * BLOCK_TOKENS_N:(g + 1) * BLOCK_TOKENS_N]
        key_portion = lax.dot_general(grad_scores, query_all, tn, preferred_element_type=jnp.float32) * scaling
        value_portion = lax.dot_general(weights, grad_all, tn, preferred_element_type=jnp.float32)
        for j in range(KEY_LIST_SIZE):
            slot = meta_ref[half, 0, j]
            keep = meta_ref[half, 1, j] != 0
            piece = slice(j * BLOCK_TOKENS_N, (j + 1) * BLOCK_TOKENS_N)
            acc_ref[slot, 0] += jnp.where(keep, key_portion[piece], 0.0)
            acc_ref[slot, 1] += jnp.where(keep, value_portion[piece], 0.0)
    for half in range(2):
        for j in range(KEY_LIST_SIZE):
            r = jnp.minimum(meta_ref[half, 0, j], seq_count - 1)
            send_ref[r] = acc_ref[r].astype(send_ref.dtype)
    own_ref[...] = acc_ref[seq_count:]


def attention_call(meta, queries, grad_out, received, mine, scaling):
    seq_count = received.shape[0]
    width = received.shape[3]
    vmem = pltpu.VMEM
    smem = pltpu.SMEM
    return pl.pallas_call(
        functools.partial(attention_kernel, scaling=scaling),
        out_shape=(
            jax.ShapeDtypeStruct(queries.shape, queries.dtype),
            jax.ShapeDtypeStruct(queries.shape, queries.dtype),
            jax.ShapeDtypeStruct(received.shape, received.dtype),
            jax.ShapeDtypeStruct((2, 2, BLOCK_TOKENS_N, width), jnp.float32),
        ),
        in_specs=[pl.BlockSpec(memory_space=smem)] + [pl.BlockSpec(memory_space=vmem)] * 4,
        out_specs=[pl.BlockSpec(memory_space=vmem)] * 4,
        scratch_shapes=[pltpu.VMEM((seq_count + 2, 2, BLOCK_TOKENS_N, width), jnp.float32)],
        compiler_params=pltpu.CompilerParams(vmem_limit_bytes=48 * 1024 * 1024),
    )(meta, queries, grad_out, received, mine)


def body(queries, key_states, value_state_rows, grad_out, layouts, plant_ids):
    scaling = HEAD_SIZE ** (-0.5)
    seq_count = lax.axis_size("seq")
    device = lax.axis_index("seq")
    count_of_blocks = layouts.shape[1]
    halfway = count_of_blocks // 2
    head_count = lax.axis_size("head")
    rows = key_states.shape[1]
    width = key_states.shape[2] // head_count
    stacked = jnp.stack([key_states, value_state_rows]).reshape(2, 2, rows, head_count, width)
    outgoing = jnp.transpose(stacked, (3, 0, 1, 2, 4))
    incoming = lax.all_to_all(outgoing, "head", split_axis=0, concat_axis=0, tiled=True)
    mine = jnp.transpose(incoming, (1, 2, 0, 3, 4)).reshape(2, 2, head_count * rows, width)
    qblocks = jnp.stack([device, count_of_blocks - 1 - device])
    pick_block = jnp.arange(count_of_blocks, dtype=jnp.int32)[None, :] == qblocks[:, None]
    plant_of = jnp.sum(jnp.where(pick_block, plant_ids[None, :], 0), axis=1)
    pick_plant = jnp.arange(layouts.shape[0], dtype=jnp.int32)[None, :] == plant_of[:, None]
    picked = pick_plant[:, :, None, None] & pick_block[:, None, :, None]
    listed_all = jnp.sum(jnp.where(picked, layouts[None], 0), axis=(1, 2))
    owners = jnp.where(listed_all < halfway, listed_all, count_of_blocks - 1 - listed_all)
    upper_half = (listed_all >= halfway).astype(jnp.int32)
    slot_of = jnp.where(owners == device, seq_count + upper_half, owners)
    live = jnp.stack([live_entries(listed_all[h]) for h in range(2)]).astype(jnp.int32)
    diagonal = (listed_all == qblocks[:, None]).astype(jnp.int32)
    meta = jnp.stack([slot_of, live, diagonal], axis=1)
    dest = jnp.arange(seq_count, dtype=jnp.int32)
    send_lower = (dest >= device)[:, None, None, None]
    send = jnp.where(send_lower, mine[:, 0][None], mine[:, 1][None])
    received = lax.all_to_all(send, "seq", split_axis=0, concat_axis=0, tiled=True)
    outputs, query_grads, partials, own = attention_call(
        meta, queries, grad_out, received, mine, scaling
    )
    back = lax.all_to_all(partials, "seq", split_axis=0, concat_axis=0, tiled=True).astype(
        jnp.float32
    )
    source = jnp.arange(seq_count, dtype=jnp.int32)
    sender_blocks = jnp.stack([source, count_of_blocks - 1 - source], axis=1)
    sender_plants = plant_ids[sender_blocks]
    sender_lists = layouts[sender_plants, sender_blocks].reshape(seq_count, -1)
    wanted = jnp.where(source > device, device, count_of_blocks - 1 - device)
    listed_here = jnp.any(sender_lists == wanted[:, None], axis=1) & (source != device)
    from_higher = (listed_here & (source > device))[:, None, None, None]
    from_lower = (listed_here & (source < device))[:, None, None, None]
    lower_total = own[0] + jnp.sum(jnp.where(from_higher, back, 0.0), axis=0)
    upper_total = own[1] + jnp.sum(jnp.where(from_lower, back, 0.0), axis=0)
    totals = jnp.stack([lower_total, upper_total], axis=1).astype(jnp.bfloat16)
    outgoing = jnp.transpose(totals.reshape(2, 2, head_count, rows, width), (2, 0, 1, 3, 4))
    incoming = lax.all_to_all(outgoing, "head", split_axis=0, concat_axis=0, tiled=True)
    grads = jnp.transpose(incoming, (1, 2, 3, 0, 4)).reshape(2, 2, rows, head_count * width)
    return (outputs, query_grads, grads[0], grads[1])


def solution(mesh):
    in_specs = (
        P(None, "seq", "head"),
        P(None, ("seq", "head"), None),
        P(None, ("seq", "head"), None),
        P(None, "seq", "head"),
        P(),
        P(),
    )
    out_specs = (
        P(None, "seq", "head"),
        P(None, "seq", "head"),
        P(None, ("seq", "head"), None),
        P(None, ("seq", "head"), None),
    )
    return jax.shard_map(body, mesh=mesh, in_specs=in_specs, out_specs=out_specs, check_vma=False)
```

```python
import jax
import jax.numpy as jnp
from jax import lax
from jax.sharding import PartitionSpec as P
import functools
from jax.experimental import pallas as pl
from jax.experimental.pallas import tpu as pltpu

HEAD_SIZE = 128
BLOCK_TOKENS_N = 64
KEY_LIST_SIZE = 8


def live_entries(listed_blocks):
    same_block = listed_blocks[:, None] == listed_blocks[None, :]
    ordinal = jnp.arange(listed_blocks.shape[0], dtype=jnp.int32)
    earlier = ordinal[None, :] < ordinal[:, None]
    return jnp.logical_not(jnp.any(same_block & earlier, axis=1))


def allowed_mask(listed_blocks, live_entry, qblock):
    offsets = jnp.arange(BLOCK_TOKENS_N, dtype=jnp.int32)
    causal = offsets[None, :] <= offsets[:, None]
    diagonal = listed_blocks == qblock
    allowed = live_entry[:, None, None] & (jnp.logical_not(diagonal)[:, None, None] | causal[None])
    return jnp.transpose(allowed, (1, 0, 2)).reshape(BLOCK_TOKENS_N, KEY_LIST_SIZE * BLOCK_TOKENS_N)


def attention_kernel(meta_ref, q_ref, do_ref, recv_ref, mine_ref,
                     out_ref, dq_ref, send_ref, own_ref, acc_ref, *, scaling):
    seq_count = recv_ref.shape[0]
    groups = q_ref.shape[2] // HEAD_SIZE
    rows = groups * BLOCK_TOKENS_N
    cols = KEY_LIST_SIZE * BLOCK_TOKENS_N
    for half in range(2):
        for j in range(KEY_LIST_SIZE):
            acc_ref[meta_ref[half, 0, j]] = jnp.zeros(acc_ref.shape[1:], acc_ref.dtype)
    col = lax.broadcasted_iota(jnp.int32, (1, cols), 1)
    col_block = col // BLOCK_TOKENS_N
    key_pos = col % BLOCK_TOKENS_N
    query_pos = lax.broadcasted_iota(jnp.int32, (rows, 1), 0) % BLOCK_TOKENS_N
    for half in range(2):
        keys, values = [], []
        live_row = jnp.zeros((1, cols), jnp.int32)
        diag_row = jnp.zeros((1, cols), jnp.int32)
        for j in range(KEY_LIST_SIZE):
            slot = meta_ref[half, 0, j]
            from_recv = slot < seq_count
            r = jnp.minimum(slot, seq_count - 1)
            m = jnp.maximum(slot - seq_count, 0)
            keys.append(jnp.where(from_recv, recv_ref[r, 0], mine_ref[0, m]))
            values.append(jnp.where(from_recv, recv_ref[r, 1], mine_ref[1, m]))
            live_row = jnp.where(col_block == j, meta_ref[half, 1, j], live_row)
            diag_row = jnp.where(col_block == j, meta_ref[half, 2, j], diag_row)
        key_all = jnp.concatenate(keys, axis=0)
        value_all = jnp.concatenate(values, axis=0)
        query_all = jnp.concatenate(
            [q_ref[half, :, g * HEAD_SIZE:(g + 1) * HEAD_SIZE] for g in range(groups)], axis=0)
        grad_all = jnp.concatenate(
            [do_ref[half, :, g * HEAD_SIZE:(g + 1) * HEAD_SIZE] for g in range(groups)], axis=0)
        allowed = (live_row != 0) & ((diag_row == 0) | (key_pos <= query_pos))
        nt = (((1,), (1,)), ((), ()))
        tn = (((0,), (0,)), ((), ()))
        scores = lax.dot_general(query_all, key_all, nt, preferred_element_type=jnp.float32) * scaling
        scores = jnp.where(allowed, scores, -1e30)
        row_max = jnp.max(scores, axis=1, keepdims=True)
        exponent = jnp.exp(scores - row_max)
        normed = exponent * (1.0 / jnp.sum(exponent, axis=1, keepdims=True))
        weights = normed.astype(jnp.bfloat16)
        block_out = jnp.dot(weights, value_all, preferred_element_type=jnp.float32).astype(out_ref.dtype)
        grad_probs = lax.dot_general(grad_all, value_all, nt, preferred_element_type=jnp.float32)
        row_delta = jnp.sum(normed * grad_probs, axis=1, keepdims=True)
        grad_scores = (normed * (grad_probs - row_delta)).astype(jnp.bfloat16)
        block_dq = (jnp.dot(grad_scores, key_all, preferred_element_type=jnp.float32) * scaling).astype(dq_ref.dtype)
        for g in range(groups):
            out_ref[half, :, g * HEAD_SIZE:(g + 1) * HEAD_SIZE] = block_out[g * BLOCK_TOKENS_N:(g + 1) * BLOCK_TOKENS_N]
            dq_ref[half, :, g * HEAD_SIZE:(g + 1) * HEAD_SIZE] = block_dq[g * BLOCK_TOKENS_N:(g + 1) * BLOCK_TOKENS_N]
        key_portion = lax.dot_general(grad_scores, query_all, tn, preferred_element_type=jnp.float32) * scaling
        value_portion = lax.dot_general(weights, grad_all, tn, preferred_element_type=jnp.float32)
        for j in range(KEY_LIST_SIZE):
            slot = meta_ref[half, 0, j]
            keep = meta_ref[half, 1, j] != 0
            piece = slice(j * BLOCK_TOKENS_N, (j + 1) * BLOCK_TOKENS_N)
            acc_ref[slot, 0] += jnp.where(keep, key_portion[piece], 0.0)
            acc_ref[slot, 1] += jnp.where(keep, value_portion[piece], 0.0)
    for half in range(2):
        for j in range(KEY_LIST_SIZE):
            r = jnp.minimum(meta_ref[half, 0, j], seq_count - 1)
            send_ref[r] = acc_ref[r].astype(send_ref.dtype)
    own_ref[...] = acc_ref[seq_count:]


def attention_call(meta, queries, grad_out, received, mine, scaling):
    seq_count = received.shape[0]
    width = received.shape[3]
    vmem = pltpu.VMEM
    smem = pltpu.SMEM
    return pl.pallas_call(
        functools.partial(attention_kernel, scaling=scaling),
        out_shape=(
            jax.ShapeDtypeStruct(queries.shape, queries.dtype),
            jax.ShapeDtypeStruct(queries.shape, queries.dtype),
            jax.ShapeDtypeStruct(received.shape, received.dtype),
            jax.ShapeDtypeStruct((2, 2, BLOCK_TOKENS_N, width), jnp.float32),
        ),
        in_specs=[pl.BlockSpec(memory_space=smem)] + [pl.BlockSpec(memory_space=vmem)] * 4,
        out_specs=[pl.BlockSpec(memory_space=vmem)] * 4,
        scratch_shapes=[pltpu.VMEM((seq_count + 2, 2, BLOCK_TOKENS_N, width), jnp.float32)],
        compiler_params=pltpu.CompilerParams(
            vmem_limit_bytes=48 * 1024 * 1024
        ),
    )(meta, queries, grad_out, received, mine)


def body(queries, key_states, value_state_rows, grad_out, layouts, plant_ids):
    scaling = HEAD_SIZE ** (-0.5)
    seq_count = lax.axis_size("seq")
    device = lax.axis_index("seq")
    count_of_blocks = layouts.shape[1]
    halfway = count_of_blocks // 2
    head_count = lax.axis_size("head")
    rows = key_states.shape[1]
    width = key_states.shape[2] // head_count
    stacked = jnp.stack([key_states, value_state_rows]).reshape(2, 2, rows, head_count, width)
    outgoing = jnp.transpose(stacked, (3, 0, 1, 2, 4))
    incoming = lax.all_to_all(outgoing, "head", split_axis=0, concat_axis=0, tiled=True)
    mine = jnp.transpose(incoming, (1, 2, 0, 3, 4)).reshape(2, 2, head_count * rows, width)
    qblocks = jnp.stack([device, count_of_blocks - 1 - device])
    pick_block = jnp.arange(count_of_blocks, dtype=jnp.int32)[None, :] == qblocks[:, None]
    plant_of = jnp.sum(jnp.where(pick_block, plant_ids[None, :], 0), axis=1)
    pick_plant = jnp.arange(layouts.shape[0], dtype=jnp.int32)[None, :] == plant_of[:, None]
    picked = pick_plant[:, :, None, None] & pick_block[:, None, :, None]
    listed_all = jnp.sum(jnp.where(picked, layouts[None], 0), axis=(1, 2))
    owners = jnp.where(listed_all < halfway, listed_all, count_of_blocks - 1 - listed_all)
    upper_half = (listed_all >= halfway).astype(jnp.int32)
    slot_of = jnp.where(owners == device, seq_count + upper_half, owners)
    live = jnp.stack([live_entries(listed_all[h]) for h in range(2)]).astype(jnp.int32)
    diagonal = (listed_all == qblocks[:, None]).astype(jnp.int32)
    meta = jnp.stack([slot_of, live, diagonal], axis=1)
    dest = jnp.arange(seq_count, dtype=jnp.int32)
    send_lower = (dest >= device)[:, None, None, None]
    send = jnp.where(send_lower, mine[:, 0][None], mine[:, 1][None])
    received = lax.all_to_all(send, "seq", split_axis=0, concat_axis=0, tiled=True)
    outputs, query_grads, partials, own = attention_call(
        meta, queries, grad_out, received, mine, scaling
    )
    back = lax.all_to_all(partials, "seq", split_axis=0, concat_axis=0, tiled=True).astype(
        jnp.float32
    )
    source = jnp.arange(seq_count, dtype=jnp.int32)
    sender_blocks = jnp.stack([source, count_of_blocks - 1 - source], axis=1)
    sender_plants = plant_ids[sender_blocks]
    sender_lists = layouts[sender_plants, sender_blocks].reshape(seq_count, -1)
    wanted = jnp.where(source > device, device, count_of_blocks - 1 - device)
    listed_here = jnp.any(sender_lists == wanted[:, None], axis=1) & (source != device)
    from_higher = (listed_here & (source > device))[:, None, None, None]
    from_lower = (listed_here & (source < device))[:, None, None, None]
    lower_total = own[0] + jnp.sum(jnp.where(from_higher, back, 0.0), axis=0)
    upper_total = own[1] + jnp.sum(jnp.where(from_lower, back, 0.0), axis=0)
    totals = jnp.stack([lower_total, upper_total], axis=1).astype(jnp.bfloat16)
    outgoing = jnp.transpose(totals.reshape(2, 2, head_count, rows, width), (2, 0, 1, 3, 4))
    incoming = lax.all_to_all(outgoing, "head", split_axis=0, concat_axis=0, tiled=True)
    grads = jnp.transpose(incoming, (1, 2, 3, 0, 4)).reshape(2, 2, rows, head_count * width)
    return (outputs, query_grads, grads[0], grads[1])


def solution(mesh):
    in_specs = (
        P(None, "seq", "head"),
        P(None, ("seq", "head"), None),
        P(None, ("seq", "head"), None),
        P(None, "seq", "head"),
        P(),
        P(),
    )
    out_specs = (
        P(None, "seq", "head"),
        P(None, "seq", "head"),
        P(None, ("seq", "head"), None),
        P(None, ("seq", "head"), None),
    )
    return jax.shard_map(body, mesh=mesh, in_specs=in_specs, out_specs=out_specs, check_vma=False)
```

```python
import jax
import jax.numpy as jnp
from jax import lax
from jax.sharding import PartitionSpec as P
import functools
from jax.experimental import pallas as pl
from jax.experimental.pallas import tpu as pltpu

HEAD_SIZE = 128
BLOCK_TOKENS_N = 64
KEY_LIST_SIZE = 8


def live_entries(listed_blocks):
    same_block = listed_blocks[:, None] == listed_blocks[None, :]
    ordinal = jnp.arange(listed_blocks.shape[0], dtype=jnp.int32)
    earlier = ordinal[None, :] < ordinal[:, None]
    return jnp.logical_not(jnp.any(same_block & earlier, axis=1))


def allowed_mask(listed_blocks, live_entry, qblock):
    offsets = jnp.arange(BLOCK_TOKENS_N, dtype=jnp.int32)
    causal = offsets[None, :] <= offsets[:, None]
    diagonal = listed_blocks == qblock
    allowed = live_entry[:, None, None] & (jnp.logical_not(diagonal)[:, None, None] | causal[None])
    return jnp.transpose(allowed, (1, 0, 2)).reshape(BLOCK_TOKENS_N, KEY_LIST_SIZE * BLOCK_TOKENS_N)


def attention_kernel(meta_ref, q_ref, do_ref, recv_ref, mine_ref,
                     out_ref, dq_ref, send_ref, own_ref, acc_ref, *, scaling):
    seq_count = recv_ref.shape[0]
    groups = q_ref.shape[2] // HEAD_SIZE
    rows = groups * BLOCK_TOKENS_N
    cols = KEY_LIST_SIZE * BLOCK_TOKENS_N
    for half in range(2):
        for j in range(KEY_LIST_SIZE):
            acc_ref[meta_ref[half, 0, j]] = jnp.zeros(acc_ref.shape[1:], acc_ref.dtype)
    col = lax.broadcasted_iota(jnp.int32, (1, cols), 1)
    col_block = col // BLOCK_TOKENS_N
    key_pos = col % BLOCK_TOKENS_N
    query_pos = lax.broadcasted_iota(jnp.int32, (BLOCK_TOKENS_N, 1), 0)
    for half in range(2):
        keys, values = [], []
        live_row = jnp.zeros((1, cols), jnp.int32)
        diag_row = jnp.zeros((1, cols), jnp.int32)
        for j in range(KEY_LIST_SIZE):
            slot = meta_ref[half, 0, j]
            from_recv = slot < seq_count
            r = jnp.minimum(slot, seq_count - 1)
            m = jnp.maximum(slot - seq_count, 0)
            keys.append(jnp.where(from_recv, recv_ref[r, 0], mine_ref[0, m]))
            values.append(jnp.where(from_recv, recv_ref[r, 1], mine_ref[1, m]))
            live_row = jnp.where(col_block == j, meta_ref[half, 1, j], live_row)
            diag_row = jnp.where(col_block == j, meta_ref[half, 2, j], diag_row)
        key_all = jnp.concatenate(keys, axis=0)
        value_all = jnp.concatenate(values, axis=0)
        allowed = (live_row != 0) & ((diag_row == 0) | (key_pos <= query_pos))
        nt = (((1,), (1,)), ((), ()))
        tn = (((0,), (0,)), ((), ()))

        def head_step(g, carry, half=half, key_all=key_all, value_all=value_all, allowed=allowed):
            key_sum, value_sum = carry
            lanes = pl.ds(pl.multiple_of(g * HEAD_SIZE, HEAD_SIZE), HEAD_SIZE)
            query_g = q_ref[half, :, lanes]
            grad_g = do_ref[half, :, lanes]
            scores = lax.dot_general(query_g, key_all, nt, preferred_element_type=jnp.float32) * scaling
            scores = jnp.where(allowed, scores, -1e30)
            row_max = jnp.max(scores, axis=1, keepdims=True)
            exponent = jnp.exp(scores - row_max)
            normed = exponent * (1.0 / jnp.sum(exponent, axis=1, keepdims=True))
            weights = normed.astype(jnp.bfloat16)
            out_ref[half, :, lanes] = jnp.dot(
                weights, value_all, preferred_element_type=jnp.float32).astype(out_ref.dtype)
            grad_probs = lax.dot_general(grad_g, value_all, nt, preferred_element_type=jnp.float32)
            row_delta = jnp.sum(normed * grad_probs, axis=1, keepdims=True)
            grad_scores = (normed * (grad_probs - row_delta)).astype(jnp.bfloat16)
            dq_ref[half, :, lanes] = (
                jnp.dot(grad_scores, key_all, preferred_element_type=jnp.float32) * scaling
            ).astype(dq_ref.dtype)
            key_sum = key_sum + lax.dot_general(grad_scores, query_g, tn, preferred_element_type=jnp.float32)
            value_sum = value_sum + lax.dot_general(weights, grad_g, tn, preferred_element_type=jnp.float32)
            return key_sum, value_sum

        zero = jnp.zeros((cols, HEAD_SIZE), jnp.float32)
        key_sum, value_sum = lax.fori_loop(0, groups, head_step, (zero, zero))
        key_portion = key_sum * scaling
        value_portion = value_sum
        for j in range(KEY_LIST_SIZE):
            slot = meta_ref[half, 0, j]
            keep = meta_ref[half, 1, j] != 0
            piece = slice(j * BLOCK_TOKENS_N, (j + 1) * BLOCK_TOKENS_N)
            acc_ref[slot, 0] += jnp.where(keep, key_portion[piece], 0.0)
            acc_ref[slot, 1] += jnp.where(keep, value_portion[piece], 0.0)
    for half in range(2):
        for j in range(KEY_LIST_SIZE):
            r = jnp.minimum(meta_ref[half, 0, j], seq_count - 1)
            send_ref[r] = acc_ref[r].astype(send_ref.dtype)
    own_ref[...] = acc_ref[seq_count:]


def attention_call(meta, queries, grad_out, received, mine, scaling):
    seq_count = received.shape[0]
    width = received.shape[3]
    vmem = pltpu.VMEM
    smem = pltpu.SMEM
    return pl.pallas_call(
        functools.partial(attention_kernel, scaling=scaling),
        out_shape=(
            jax.ShapeDtypeStruct(queries.shape, queries.dtype),
            jax.ShapeDtypeStruct(queries.shape, queries.dtype),
            jax.ShapeDtypeStruct(received.shape, received.dtype),
            jax.ShapeDtypeStruct((2, 2, BLOCK_TOKENS_N, width), jnp.float32),
        ),
        in_specs=[pl.BlockSpec(memory_space=smem)] + [pl.BlockSpec(memory_space=vmem)] * 4,
        out_specs=[pl.BlockSpec(memory_space=vmem)] * 4,
        scratch_shapes=[pltpu.VMEM((seq_count + 2, 2, BLOCK_TOKENS_N, width), jnp.float32)],
        compiler_params=pltpu.CompilerParams(
            vmem_limit_bytes=48 * 1024 * 1024
        ),
    )(meta, queries, grad_out, received, mine)


def body(queries, key_states, value_state_rows, grad_out, layouts, plant_ids):
    scaling = HEAD_SIZE ** (-0.5)
    seq_count = lax.axis_size("seq")
    device = lax.axis_index("seq")
    count_of_blocks = layouts.shape[1]
    halfway = count_of_blocks // 2
    head_count = lax.axis_size("head")
    rows = key_states.shape[1]
    width = key_states.shape[2] // head_count
    stacked = jnp.stack([key_states, value_state_rows]).reshape(2, 2, rows, head_count, width)
    outgoing = jnp.transpose(stacked, (3, 0, 1, 2, 4))
    incoming = lax.all_to_all(outgoing, "head", split_axis=0, concat_axis=0, tiled=True)
    mine = jnp.transpose(incoming, (1, 2, 0, 3, 4)).reshape(2, 2, head_count * rows, width)
    qblocks = jnp.stack([device, count_of_blocks - 1 - device])
    pick_block = jnp.arange(count_of_blocks, dtype=jnp.int32)[None, :] == qblocks[:, None]
    plant_of = jnp.sum(jnp.where(pick_block, plant_ids[None, :], 0), axis=1)
    pick_plant = jnp.arange(layouts.shape[0], dtype=jnp.int32)[None, :] == plant_of[:, None]
    picked = pick_plant[:, :, None, None] & pick_block[:, None, :, None]
    listed_all = jnp.sum(jnp.where(picked, layouts[None], 0), axis=(1, 2))
    owners = jnp.where(listed_all < halfway, listed_all, count_of_blocks - 1 - listed_all)
    upper_half = (listed_all >= halfway).astype(jnp.int32)
    slot_of = jnp.where(owners == device, seq_count + upper_half, owners)
    live = jnp.stack([live_entries(listed_all[h]) for h in range(2)]).astype(jnp.int32)
    diagonal = (listed_all == qblocks[:, None]).astype(jnp.int32)
    meta = jnp.stack([slot_of, live, diagonal], axis=1)
    dest = jnp.arange(seq_count, dtype=jnp.int32)
    send_lower = (dest >= device)[:, None, None, None]
    send = jnp.where(send_lower, mine[:, 0][None], mine[:, 1][None])
    received = lax.all_to_all(send, "seq", split_axis=0, concat_axis=0, tiled=True)
    outputs, query_grads, partials, own = attention_call(
        meta, queries, grad_out, received, mine, scaling
    )
    back = lax.all_to_all(partials, "seq", split_axis=0, concat_axis=0, tiled=True).astype(
        jnp.float32
    )
    source = jnp.arange(seq_count, dtype=jnp.int32)
    sender_blocks = jnp.stack([source, count_of_blocks - 1 - source], axis=1)
    sender_plants = plant_ids[sender_blocks]
    sender_lists = layouts[sender_plants, sender_blocks].reshape(seq_count, -1)
    wanted = jnp.where(source > device, device, count_of_blocks - 1 - device)
    listed_here = jnp.any(sender_lists == wanted[:, None], axis=1) & (source != device)
    from_higher = (listed_here & (source > device))[:, None, None, None]
    from_lower = (listed_here & (source < device))[:, None, None, None]
    lower_total = own[0] + jnp.sum(jnp.where(from_higher, back, 0.0), axis=0)
    upper_total = own[1] + jnp.sum(jnp.where(from_lower, back, 0.0), axis=0)
    totals = jnp.stack([lower_total, upper_total], axis=1).astype(jnp.bfloat16)
    outgoing = jnp.transpose(totals.reshape(2, 2, head_count, rows, width), (2, 0, 1, 3, 4))
    incoming = lax.all_to_all(outgoing, "head", split_axis=0, concat_axis=0, tiled=True)
    grads = jnp.transpose(incoming, (1, 2, 3, 0, 4)).reshape(2, 2, rows, head_count * width)
    return (outputs, query_grads, grads[0], grads[1])


def solution(mesh):
    in_specs = (
        P(None, "seq", "head"),
        P(None, ("seq", "head"), None),
        P(None, ("seq", "head"), None),
        P(None, "seq", "head"),
        P(),
        P(),
    )
    out_specs = (
        P(None, "seq", "head"),
        P(None, "seq", "head"),
        P(None, ("seq", "head"), None),
        P(None, ("seq", "head"), None),
    )
    return jax.shard_map(body, mesh=mesh, in_specs=in_specs, out_specs=out_specs, check_vma=False)
```

```python
import jax
import jax.numpy as jnp
from jax import lax
from jax.sharding import PartitionSpec as P
import functools
from jax.experimental import pallas as pl
from jax.experimental.pallas import tpu as pltpu

HEAD_SIZE = 128
BLOCK_TOKENS_N = 64
KEY_LIST_SIZE = 8


def live_entries(listed_blocks):
    same_block = listed_blocks[:, None] == listed_blocks[None, :]
    ordinal = jnp.arange(listed_blocks.shape[0], dtype=jnp.int32)
    earlier = ordinal[None, :] < ordinal[:, None]
    return jnp.logical_not(jnp.any(same_block & earlier, axis=1))


def allowed_mask(listed_blocks, live_entry, qblock):
    offsets = jnp.arange(BLOCK_TOKENS_N, dtype=jnp.int32)
    causal = offsets[None, :] <= offsets[:, None]
    diagonal = listed_blocks == qblock
    allowed = live_entry[:, None, None] & (jnp.logical_not(diagonal)[:, None, None] | causal[None])
    return jnp.transpose(allowed, (1, 0, 2)).reshape(BLOCK_TOKENS_N, KEY_LIST_SIZE * BLOCK_TOKENS_N)


def attention_kernel(meta_ref, q_ref, do_ref, recv_ref, mine_ref,
                     send_ref, own_ref, w_ref, ds_ref, k_ref, v_ref, acc_ref, *, scaling):
    seq_count = recv_ref.shape[0]
    groups = q_ref.shape[2] // HEAD_SIZE
    rows = groups * BLOCK_TOKENS_N
    cols = KEY_LIST_SIZE * BLOCK_TOKENS_N
    for half in range(2):
        for j in range(KEY_LIST_SIZE):
            acc_ref[meta_ref[half, 0, j]] = jnp.zeros(acc_ref.shape[1:], acc_ref.dtype)
    col = lax.broadcasted_iota(jnp.int32, (1, cols), 1)
    col_block = col // BLOCK_TOKENS_N
    key_pos = col % BLOCK_TOKENS_N
    query_pos = lax.broadcasted_iota(jnp.int32, (rows, 1), 0) % BLOCK_TOKENS_N
    for half in range(2):
        keys, values = [], []
        live_row = jnp.zeros((1, cols), jnp.int32)
        diag_row = jnp.zeros((1, cols), jnp.int32)
        for j in range(KEY_LIST_SIZE):
            slot = meta_ref[half, 0, j]
            from_recv = slot < seq_count
            r = jnp.minimum(slot, seq_count - 1)
            m = jnp.maximum(slot - seq_count, 0)
            keys.append(jnp.where(from_recv, recv_ref[r, 0], mine_ref[0, m]))
            values.append(jnp.where(from_recv, recv_ref[r, 1], mine_ref[1, m]))
            live_row = jnp.where(col_block == j, meta_ref[half, 1, j], live_row)
            diag_row = jnp.where(col_block == j, meta_ref[half, 2, j], diag_row)
        key_all = jnp.concatenate(keys, axis=0)
        value_all = jnp.concatenate(values, axis=0)
        query_all = jnp.concatenate(
            [q_ref[half, :, g * HEAD_SIZE:(g + 1) * HEAD_SIZE] for g in range(groups)], axis=0)
        grad_all = jnp.concatenate(
            [do_ref[half, :, g * HEAD_SIZE:(g + 1) * HEAD_SIZE] for g in range(groups)], axis=0)
        allowed = (live_row != 0) & ((diag_row == 0) | (key_pos <= query_pos))
        nt = (((1,), (1,)), ((), ()))
        tn = (((0,), (0,)), ((), ()))
        scores = lax.dot_general(query_all, key_all, nt, preferred_element_type=jnp.float32) * scaling
        scores = jnp.where(allowed, scores, -1e30)
        row_max = jnp.max(scores, axis=1, keepdims=True)
        exponent = jnp.exp(scores - row_max)
        normed = exponent * (1.0 / jnp.sum(exponent, axis=1, keepdims=True))
        weights = normed.astype(jnp.bfloat16)
        grad_probs = lax.dot_general(grad_all, value_all, nt, preferred_element_type=jnp.float32)
        row_delta = jnp.sum(normed * grad_probs, axis=1, keepdims=True)
        grad_scores = (normed * (grad_probs - row_delta)).astype(jnp.bfloat16)
        w_ref[half] = weights
        ds_ref[half] = grad_scores
        k_ref[half] = key_all
        v_ref[half] = value_all
        key_portion = lax.dot_general(grad_scores, query_all, tn, preferred_element_type=jnp.float32) * scaling
        value_portion = lax.dot_general(weights, grad_all, tn, preferred_element_type=jnp.float32)
        for j in range(KEY_LIST_SIZE):
            slot = meta_ref[half, 0, j]
            keep = meta_ref[half, 1, j] != 0
            piece = slice(j * BLOCK_TOKENS_N, (j + 1) * BLOCK_TOKENS_N)
            acc_ref[slot, 0] += jnp.where(keep, key_portion[piece], 0.0)
            acc_ref[slot, 1] += jnp.where(keep, value_portion[piece], 0.0)
    for half in range(2):
        for j in range(KEY_LIST_SIZE):
            r = jnp.minimum(meta_ref[half, 0, j], seq_count - 1)
            send_ref[r] = acc_ref[r].astype(send_ref.dtype)
    own_ref[...] = acc_ref[seq_count:]


def output_kernel(w_ref, ds_ref, k_ref, v_ref, out_ref, dq_ref, *, scaling):
    groups = out_ref.shape[2] // HEAD_SIZE
    for half in range(2):
        block_out = jnp.dot(w_ref[half], v_ref[half], preferred_element_type=jnp.float32).astype(out_ref.dtype)
        block_dq = (jnp.dot(ds_ref[half], k_ref[half], preferred_element_type=jnp.float32) * scaling).astype(dq_ref.dtype)
        for g in range(groups):
            out_ref[half, :, g * HEAD_SIZE:(g + 1) * HEAD_SIZE] = block_out[g * BLOCK_TOKENS_N:(g + 1) * BLOCK_TOKENS_N]
            dq_ref[half, :, g * HEAD_SIZE:(g + 1) * HEAD_SIZE] = block_dq[g * BLOCK_TOKENS_N:(g + 1) * BLOCK_TOKENS_N]


def attention_call(meta, queries, grad_out, received, mine, scaling):
    seq_count = received.shape[0]
    width = received.shape[3]
    groups = queries.shape[2] // HEAD_SIZE
    rows = groups * BLOCK_TOKENS_N
    cols = KEY_LIST_SIZE * BLOCK_TOKENS_N
    vmem = pltpu.VMEM
    smem = pltpu.SMEM
    send, own, weights, grad_scores, keys, values = pl.pallas_call(
        functools.partial(attention_kernel, scaling=scaling),
        out_shape=(
            jax.ShapeDtypeStruct(received.shape, received.dtype),
            jax.ShapeDtypeStruct((2, 2, BLOCK_TOKENS_N, width), jnp.float32),
            jax.ShapeDtypeStruct((2, rows, cols), jnp.bfloat16),
            jax.ShapeDtypeStruct((2, rows, cols), jnp.bfloat16),
            jax.ShapeDtypeStruct((2, cols, width), received.dtype),
            jax.ShapeDtypeStruct((2, cols, width), received.dtype),
        ),
        in_specs=[pl.BlockSpec(memory_space=smem)] + [pl.BlockSpec(memory_space=vmem)] * 4,
        out_specs=[pl.BlockSpec(memory_space=vmem)] * 6,
        scratch_shapes=[pltpu.VMEM((seq_count + 2, 2, BLOCK_TOKENS_N, width), jnp.float32)],
        compiler_params=pltpu.CompilerParams(
            vmem_limit_bytes=48 * 1024 * 1024
        ),
        cost_estimate=pl.CostEstimate(flops=1600000000, bytes_accessed=8000000, transcendentals=524288),
    )(meta, queries, grad_out, received, mine)
    outputs, query_grads = pl.pallas_call(
        functools.partial(output_kernel, scaling=scaling),
        out_shape=(
            jax.ShapeDtypeStruct(queries.shape, queries.dtype),
            jax.ShapeDtypeStruct(queries.shape, queries.dtype),
        ),
        in_specs=[pl.BlockSpec(memory_space=vmem)] * 4,
        out_specs=[pl.BlockSpec(memory_space=vmem)] * 2,
        compiler_params=pltpu.CompilerParams(vmem_limit_bytes=32 * 1024 * 1024),
        cost_estimate=pl.CostEstimate(flops=536870912, bytes_accessed=2500000, transcendentals=0),
    )(weights, grad_scores, keys, values)
    return outputs, query_grads, send, own


def body(queries, key_states, value_state_rows, grad_out, layouts, plant_ids):
    scaling = HEAD_SIZE ** (-0.5)
    seq_count = lax.axis_size("seq")
    device = lax.axis_index("seq")
    count_of_blocks = layouts.shape[1]
    halfway = count_of_blocks // 2
    head_count = lax.axis_size("head")
    rows = key_states.shape[1]
    width = key_states.shape[2] // head_count
    stacked = jnp.stack([key_states, value_state_rows]).reshape(2, 2, rows, head_count, width)
    outgoing = jnp.transpose(stacked, (3, 0, 1, 2, 4))
    incoming = lax.all_to_all(outgoing, "head", split_axis=0, concat_axis=0, tiled=True)
    mine = jnp.transpose(incoming, (1, 2, 0, 3, 4)).reshape(2, 2, head_count * rows, width)
    qblocks = jnp.stack([device, count_of_blocks - 1 - device])
    pick_block = jnp.arange(count_of_blocks, dtype=jnp.int32)[None, :] == qblocks[:, None]
    plant_of = jnp.sum(jnp.where(pick_block, plant_ids[None, :], 0), axis=1)
    pick_plant = jnp.arange(layouts.shape[0], dtype=jnp.int32)[None, :] == plant_of[:, None]
    picked = pick_plant[:, :, None, None] & pick_block[:, None, :, None]
    listed_all = jnp.sum(jnp.where(picked, layouts[None], 0), axis=(1, 2))
    owners = jnp.where(listed_all < halfway, listed_all, count_of_blocks - 1 - listed_all)
    upper_half = (listed_all >= halfway).astype(jnp.int32)
    slot_of = jnp.where(owners == device, seq_count + upper_half, owners)
    live = jnp.stack([live_entries(listed_all[h]) for h in range(2)]).astype(jnp.int32)
    diagonal = (listed_all == qblocks[:, None]).astype(jnp.int32)
    meta = jnp.stack([slot_of, live, diagonal], axis=1)
    dest = jnp.arange(seq_count, dtype=jnp.int32)
    send_lower = (dest >= device)[:, None, None, None]
    send = jnp.where(send_lower, mine[:, 0][None], mine[:, 1][None])
    received = lax.all_to_all(send, "seq", split_axis=0, concat_axis=0, tiled=True)
    outputs, query_grads, partials, own = attention_call(
        meta, queries, grad_out, received, mine, scaling
    )
    back = lax.all_to_all(partials, "seq", split_axis=0, concat_axis=0, tiled=True).astype(
        jnp.float32
    )
    source = jnp.arange(seq_count, dtype=jnp.int32)
    sender_blocks = jnp.stack([source, count_of_blocks - 1 - source], axis=1)
    sender_plants = plant_ids[sender_blocks]
    sender_lists = layouts[sender_plants, sender_blocks].reshape(seq_count, -1)
    wanted = jnp.where(source > device, device, count_of_blocks - 1 - device)
    listed_here = jnp.any(sender_lists == wanted[:, None], axis=1) & (source != device)
    from_higher = (listed_here & (source > device))[:, None, None, None]
    from_lower = (listed_here & (source < device))[:, None, None, None]
    lower_total = own[0] + jnp.sum(jnp.where(from_higher, back, 0.0), axis=0)
    upper_total = own[1] + jnp.sum(jnp.where(from_lower, back, 0.0), axis=0)
    totals = jnp.stack([lower_total, upper_total], axis=1).astype(jnp.bfloat16)
    outgoing = jnp.transpose(totals.reshape(2, 2, head_count, rows, width), (2, 0, 1, 3, 4))
    incoming = lax.all_to_all(outgoing, "head", split_axis=0, concat_axis=0, tiled=True)
    grads = jnp.transpose(incoming, (1, 2, 3, 0, 4)).reshape(2, 2, rows, head_count * width)
    return (outputs, query_grads, grads[0], grads[1])


def solution(mesh):
    in_specs = (
        P(None, "seq", "head"),
        P(None, ("seq", "head"), None),
        P(None, ("seq", "head"), None),
        P(None, "seq", "head"),
        P(),
        P(),
    )
    out_specs = (
        P(None, "seq", "head"),
        P(None, "seq", "head"),
        P(None, ("seq", "head"), None),
        P(None, ("seq", "head"), None),
    )
    return jax.shard_map(body, mesh=mesh, in_specs=in_specs, out_specs=out_specs, check_vma=False)
```

```python
import jax
import jax.numpy as jnp
from jax import lax
from jax.sharding import PartitionSpec as P
import functools
from jax.experimental import pallas as pl
from jax.experimental.pallas import tpu as pltpu

HEAD_SIZE = 128
BLOCK_TOKENS_N = 64
KEY_LIST_SIZE = 8


def live_entries(listed_blocks):
    same_block = listed_blocks[:, None] == listed_blocks[None, :]
    ordinal = jnp.arange(listed_blocks.shape[0], dtype=jnp.int32)
    earlier = ordinal[None, :] < ordinal[:, None]
    return jnp.logical_not(jnp.any(same_block & earlier, axis=1))


def allowed_mask(listed_blocks, live_entry, qblock):
    offsets = jnp.arange(BLOCK_TOKENS_N, dtype=jnp.int32)
    causal = offsets[None, :] <= offsets[:, None]
    diagonal = listed_blocks == qblock
    allowed = live_entry[:, None, None] & (jnp.logical_not(diagonal)[:, None, None] | causal[None])
    return jnp.transpose(allowed, (1, 0, 2)).reshape(BLOCK_TOKENS_N, KEY_LIST_SIZE * BLOCK_TOKENS_N)


def attention_kernel(meta_ref, q_ref, do_ref, recv_ref, mine_ref,
                     out_ref, dq_ref, send_ref, own_ref, acc_ref, *, scaling):
    seq_count = recv_ref.shape[0]
    groups = q_ref.shape[2] // HEAD_SIZE
    rows = groups * BLOCK_TOKENS_N
    cols = KEY_LIST_SIZE * BLOCK_TOKENS_N
    for half in range(2):
        for j in range(KEY_LIST_SIZE):
            acc_ref[meta_ref[half, 0, j]] = jnp.zeros(acc_ref.shape[1:], acc_ref.dtype)
    col = lax.broadcasted_iota(jnp.int32, (1, cols), 1)
    col_block = col // BLOCK_TOKENS_N
    key_pos = col % BLOCK_TOKENS_N
    query_pos = lax.broadcasted_iota(jnp.int32, (rows, 1), 0) % BLOCK_TOKENS_N
    causal_bias = jnp.where((col >= BLOCK_TOKENS_N) | (key_pos <= query_pos), 0.0, -1e30)
    for half in range(2):
        keys, values = [], []
        live_row = jnp.zeros((1, cols), jnp.int32)
        for j in range(KEY_LIST_SIZE):
            slot = meta_ref[half, 0, j]
            from_recv = slot < seq_count
            r = jnp.minimum(slot, seq_count - 1)
            m = jnp.maximum(slot - seq_count, 0)
            keys.append(jnp.where(from_recv, recv_ref[r, 0], mine_ref[0, m]))
            values.append(jnp.where(from_recv, recv_ref[r, 1], mine_ref[1, m]))
            live_row = jnp.where(col_block == j, meta_ref[half, 1, j], live_row)
        key_all = jnp.concatenate(keys, axis=0)
        value_all = jnp.concatenate(values, axis=0)
        query_all = jnp.concatenate(
            [q_ref[half, :, g * HEAD_SIZE:(g + 1) * HEAD_SIZE] for g in range(groups)], axis=0)
        grad_all = jnp.concatenate(
            [do_ref[half, :, g * HEAD_SIZE:(g + 1) * HEAD_SIZE] for g in range(groups)], axis=0)
        live_bias = jnp.where(live_row != 0, 0.0, -1e30)
        nt = (((1,), (1,)), ((), ()))
        tn = (((0,), (0,)), ((), ()))
        scores = lax.dot_general(query_all, key_all, nt, preferred_element_type=jnp.float32) * scaling
        scores = scores + causal_bias + live_bias
        row_max = jnp.max(scores, axis=1, keepdims=True)
        exponent = jnp.exp(scores - row_max)
        normed = exponent * (1.0 / jnp.sum(exponent, axis=1, keepdims=True))
        weights = normed.astype(jnp.bfloat16)
        block_out = jnp.dot(weights, value_all, preferred_element_type=jnp.float32).astype(out_ref.dtype)
        grad_probs = lax.dot_general(grad_all, value_all, nt, preferred_element_type=jnp.float32)
        row_delta = jnp.sum(normed * grad_probs, axis=1, keepdims=True)
        grad_scores = (normed * (grad_probs - row_delta)).astype(jnp.bfloat16)
        block_dq = (jnp.dot(grad_scores, key_all, preferred_element_type=jnp.float32) * scaling).astype(dq_ref.dtype)
        for g in range(groups):
            out_ref[half, :, g * HEAD_SIZE:(g + 1) * HEAD_SIZE] = block_out[g * BLOCK_TOKENS_N:(g + 1) * BLOCK_TOKENS_N]
            dq_ref[half, :, g * HEAD_SIZE:(g + 1) * HEAD_SIZE] = block_dq[g * BLOCK_TOKENS_N:(g + 1) * BLOCK_TOKENS_N]
        key_portion = lax.dot_general(grad_scores, query_all, tn, preferred_element_type=jnp.float32) * scaling
        value_portion = lax.dot_general(weights, grad_all, tn, preferred_element_type=jnp.float32)
        for j in range(KEY_LIST_SIZE):
            slot = meta_ref[half, 0, j]
            keep = meta_ref[half, 1, j] != 0
            piece = slice(j * BLOCK_TOKENS_N, (j + 1) * BLOCK_TOKENS_N)
            acc_ref[slot, 0] += jnp.where(keep, key_portion[piece], 0.0)
            acc_ref[slot, 1] += jnp.where(keep, value_portion[piece], 0.0)
    for half in range(2):
        for j in range(KEY_LIST_SIZE):
            r = jnp.minimum(meta_ref[half, 0, j], seq_count - 1)
            send_ref[r] = acc_ref[r].astype(send_ref.dtype)
    own_ref[...] = acc_ref[seq_count:]


def attention_call(meta, queries, grad_out, received, mine, scaling):
    seq_count = received.shape[0]
    width = received.shape[3]
    vmem = pltpu.VMEM
    smem = pltpu.SMEM
    return pl.pallas_call(
        functools.partial(attention_kernel, scaling=scaling),
        out_shape=(
            jax.ShapeDtypeStruct(queries.shape, queries.dtype),
            jax.ShapeDtypeStruct(queries.shape, queries.dtype),
            jax.ShapeDtypeStruct(received.shape, received.dtype),
            jax.ShapeDtypeStruct((2, 2, BLOCK_TOKENS_N, width), jnp.float32),
        ),
        in_specs=[pl.BlockSpec(memory_space=smem)] + [pl.BlockSpec(memory_space=vmem)] * 4,
        out_specs=[pl.BlockSpec(memory_space=vmem)] * 4,
        scratch_shapes=[pltpu.VMEM((seq_count + 2, 2, BLOCK_TOKENS_N, width), jnp.float32)],
        compiler_params=pltpu.CompilerParams(
            vmem_limit_bytes=48 * 1024 * 1024
        ),
    )(meta, queries, grad_out, received, mine)


def body(queries, key_states, value_state_rows, grad_out, layouts, plant_ids):
    scaling = HEAD_SIZE ** (-0.5)
    seq_count = lax.axis_size("seq")
    device = lax.axis_index("seq")
    count_of_blocks = layouts.shape[1]
    halfway = count_of_blocks // 2
    head_count = lax.axis_size("head")
    rows = key_states.shape[1]
    width = key_states.shape[2] // head_count
    stacked = jnp.stack([key_states, value_state_rows]).reshape(2, 2, rows, head_count, width)
    outgoing = jnp.transpose(stacked, (3, 0, 1, 2, 4))
    incoming = lax.all_to_all(outgoing, "head", split_axis=0, concat_axis=0, tiled=True)
    mine = jnp.transpose(incoming, (1, 2, 0, 3, 4)).reshape(2, 2, head_count * rows, width)
    qblocks = jnp.stack([device, count_of_blocks - 1 - device])
    pick_block = jnp.arange(count_of_blocks, dtype=jnp.int32)[None, :] == qblocks[:, None]
    plant_of = jnp.sum(jnp.where(pick_block, plant_ids[None, :], 0), axis=1)
    pick_plant = jnp.arange(layouts.shape[0], dtype=jnp.int32)[None, :] == plant_of[:, None]
    picked = pick_plant[:, :, None, None] & pick_block[:, None, :, None]
    listed_all = jnp.sum(jnp.where(picked, layouts[None], 0), axis=(1, 2))
    owners = jnp.where(listed_all < halfway, listed_all, count_of_blocks - 1 - listed_all)
    upper_half = (listed_all >= halfway).astype(jnp.int32)
    slot_of = jnp.where(owners == device, seq_count + upper_half, owners)
    live = jnp.stack([live_entries(listed_all[h]) for h in range(2)]).astype(jnp.int32)
    diagonal = (listed_all == qblocks[:, None]).astype(jnp.int32)
    meta = jnp.stack([slot_of, live, diagonal], axis=1)
    dest = jnp.arange(seq_count, dtype=jnp.int32)
    send_lower = (dest >= device)[:, None, None, None]
    send = jnp.where(send_lower, mine[:, 0][None], mine[:, 1][None])
    received = lax.all_to_all(send, "seq", split_axis=0, concat_axis=0, tiled=True)
    outputs, query_grads, partials, own = attention_call(
        meta, queries, grad_out, received, mine, scaling
    )
    back = lax.all_to_all(partials, "seq", split_axis=0, concat_axis=0, tiled=True).astype(
        jnp.float32
    )
    source = jnp.arange(seq_count, dtype=jnp.int32)
    sender_blocks = jnp.stack([source, count_of_blocks - 1 - source], axis=1)
    sender_plants = plant_ids[sender_blocks]
    sender_lists = layouts[sender_plants, sender_blocks].reshape(seq_count, -1)
    wanted = jnp.where(source > device, device, count_of_blocks - 1 - device)
    listed_here = jnp.any(sender_lists == wanted[:, None], axis=1) & (source != device)
    from_higher = (listed_here & (source > device))[:, None, None, None]
    from_lower = (listed_here & (source < device))[:, None, None, None]
    lower_total = own[0] + jnp.sum(jnp.where(from_higher, back, 0.0), axis=0)
    upper_total = own[1] + jnp.sum(jnp.where(from_lower, back, 0.0), axis=0)
    totals = jnp.stack([lower_total, upper_total], axis=1).astype(jnp.bfloat16)
    outgoing = jnp.transpose(totals.reshape(2, 2, head_count, rows, width), (2, 0, 1, 3, 4))
    incoming = lax.all_to_all(outgoing, "head", split_axis=0, concat_axis=0, tiled=True)
    grads = jnp.transpose(incoming, (1, 2, 3, 0, 4)).reshape(2, 2, rows, head_count * width)
    return (outputs, query_grads, grads[0], grads[1])


def solution(mesh):
    in_specs = (
        P(None, "seq", "head"),
        P(None, ("seq", "head"), None),
        P(None, ("seq", "head"), None),
        P(None, "seq", "head"),
        P(),
        P(),
    )
    out_specs = (
        P(None, "seq", "head"),
        P(None, "seq", "head"),
        P(None, ("seq", "head"), None),
        P(None, ("seq", "head"), None),
    )
    return jax.shard_map(body, mesh=mesh, in_specs=in_specs, out_specs=out_specs, check_vma=False)
```

```python
import jax
import jax.numpy as jnp
from jax import lax
from jax.sharding import PartitionSpec as P
import functools
from jax.experimental import pallas as pl
from jax.experimental.pallas import tpu as pltpu

HEAD_SIZE = 128
BLOCK_TOKENS_N = 64
KEY_LIST_SIZE = 8


def live_entries(listed_blocks):
    same_block = listed_blocks[:, None] == listed_blocks[None, :]
    ordinal = jnp.arange(listed_blocks.shape[0], dtype=jnp.int32)
    earlier = ordinal[None, :] < ordinal[:, None]
    return jnp.logical_not(jnp.any(same_block & earlier, axis=1))


def allowed_mask(listed_blocks, live_entry, qblock):
    offsets = jnp.arange(BLOCK_TOKENS_N, dtype=jnp.int32)
    causal = offsets[None, :] <= offsets[:, None]
    diagonal = listed_blocks == qblock
    allowed = live_entry[:, None, None] & (jnp.logical_not(diagonal)[:, None, None] | causal[None])
    return jnp.transpose(allowed, (1, 0, 2)).reshape(BLOCK_TOKENS_N, KEY_LIST_SIZE * BLOCK_TOKENS_N)


def attention_kernel(meta_ref, q_ref, do_ref, recv_ref, mine_ref,
                     out_ref, dq_ref, send_ref, own_ref, acc_ref, *, scaling):
    seq_count = recv_ref.shape[0]
    groups = q_ref.shape[2] // HEAD_SIZE
    rows = groups * BLOCK_TOKENS_N
    cols = KEY_LIST_SIZE * BLOCK_TOKENS_N
    col = lax.broadcasted_iota(jnp.int32, (1, cols), 1)
    col_block = col // BLOCK_TOKENS_N
    key_pos = col % BLOCK_TOKENS_N
    query_pos = lax.broadcasted_iota(jnp.int32, (rows, 1), 0) % BLOCK_TOKENS_N
    causal_bias = jnp.where((col >= BLOCK_TOKENS_N) | (key_pos <= query_pos), 0.0, -1e30)
    for half in range(2):
        keys, values = [], []
        live_row = jnp.zeros((1, cols), jnp.int32)
        for j in range(KEY_LIST_SIZE):
            slot = meta_ref[half, 0, j]
            from_recv = slot < seq_count
            r = jnp.minimum(slot, seq_count - 1)
            m = jnp.maximum(slot - seq_count, 0)
            keys.append(jnp.where(from_recv, recv_ref[r, 0], mine_ref[0, m]))
            values.append(jnp.where(from_recv, recv_ref[r, 1], mine_ref[1, m]))
            live_row = jnp.where(col_block == j, meta_ref[half, 1, j], live_row)
        key_all = jnp.concatenate(keys, axis=0)
        value_all = jnp.concatenate(values, axis=0)
        query_all = jnp.concatenate(
            [q_ref[half, :, g * HEAD_SIZE:(g + 1) * HEAD_SIZE] for g in range(groups)], axis=0)
        grad_all = jnp.concatenate(
            [do_ref[half, :, g * HEAD_SIZE:(g + 1) * HEAD_SIZE] for g in range(groups)], axis=0)
        live_bias = jnp.where(live_row != 0, 0.0, -1e30)
        nt = (((1,), (1,)), ((), ()))
        tn = (((0,), (0,)), ((), ()))
        scores = lax.dot_general(query_all, key_all, nt, preferred_element_type=jnp.float32) * scaling
        scores = scores + causal_bias + live_bias
        row_max = jnp.max(scores, axis=1, keepdims=True)
        exponent = jnp.exp(scores - row_max)
        normed = exponent * (1.0 / jnp.sum(exponent, axis=1, keepdims=True))
        weights = normed.astype(jnp.bfloat16)
        block_out = jnp.dot(weights, value_all, preferred_element_type=jnp.float32).astype(out_ref.dtype)
        grad_probs = lax.dot_general(grad_all, value_all, nt, preferred_element_type=jnp.float32)
        row_delta = jnp.sum(normed * grad_probs, axis=1, keepdims=True)
        grad_scores = (normed * (grad_probs - row_delta)).astype(jnp.bfloat16)
        block_dq = (jnp.dot(grad_scores, key_all, preferred_element_type=jnp.float32) * scaling).astype(dq_ref.dtype)
        for g in range(groups):
            out_ref[half, :, g * HEAD_SIZE:(g + 1) * HEAD_SIZE] = block_out[g * BLOCK_TOKENS_N:(g + 1) * BLOCK_TOKENS_N]
            dq_ref[half, :, g * HEAD_SIZE:(g + 1) * HEAD_SIZE] = block_dq[g * BLOCK_TOKENS_N:(g + 1) * BLOCK_TOKENS_N]
        key_portion = lax.dot_general(grad_scores, query_all, tn, preferred_element_type=jnp.float32) * scaling
        value_portion = lax.dot_general(weights, grad_all, tn, preferred_element_type=jnp.float32)
        for j in range(KEY_LIST_SIZE):
            slot = meta_ref[half, 0, j]
            keep = meta_ref[half, 1, j] != 0
            piece = slice(j * BLOCK_TOKENS_N, (j + 1) * BLOCK_TOKENS_N)
            first = meta_ref[half, 2, j] != 0
            key_piece = key_portion[piece]
            value_piece = value_portion[piece]

            @pl.when(keep & first)
            def _():
                acc_ref[slot, 0] = key_piece
                acc_ref[slot, 1] = value_piece

            @pl.when(keep & jnp.logical_not(first))
            def _():
                acc_ref[slot, 0] += key_piece
                acc_ref[slot, 1] += value_piece
    for half in range(2):
        for j in range(KEY_LIST_SIZE):
            r = jnp.minimum(meta_ref[half, 0, j], seq_count - 1)
            send_ref[r] = acc_ref[r].astype(send_ref.dtype)
    own_ref[...] = acc_ref[seq_count:]


def attention_call(meta, queries, grad_out, received, mine, scaling):
    seq_count = received.shape[0]
    width = received.shape[3]
    vmem = pltpu.VMEM
    smem = pltpu.SMEM
    return pl.pallas_call(
        functools.partial(attention_kernel, scaling=scaling),
        out_shape=(
            jax.ShapeDtypeStruct(queries.shape, queries.dtype),
            jax.ShapeDtypeStruct(queries.shape, queries.dtype),
            jax.ShapeDtypeStruct(received.shape, received.dtype),
            jax.ShapeDtypeStruct((2, 2, BLOCK_TOKENS_N, width), jnp.float32),
        ),
        in_specs=[pl.BlockSpec(memory_space=smem)] + [pl.BlockSpec(memory_space=vmem)] * 4,
        out_specs=[pl.BlockSpec(memory_space=vmem)] * 4,
        scratch_shapes=[pltpu.VMEM((seq_count + 2, 2, BLOCK_TOKENS_N, width), jnp.float32)],
        compiler_params=pltpu.CompilerParams(
            vmem_limit_bytes=48 * 1024 * 1024
        ),
    )(meta, queries, grad_out, received, mine)


def body(queries, key_states, value_state_rows, grad_out, layouts, plant_ids):
    scaling = HEAD_SIZE ** (-0.5)
    seq_count = lax.axis_size("seq")
    device = lax.axis_index("seq")
    count_of_blocks = layouts.shape[1]
    halfway = count_of_blocks // 2
    head_count = lax.axis_size("head")
    rows = key_states.shape[1]
    width = key_states.shape[2] // head_count
    stacked = jnp.stack([key_states, value_state_rows]).reshape(2, 2, rows, head_count, width)
    outgoing = jnp.transpose(stacked, (3, 0, 1, 2, 4))
    incoming = lax.all_to_all(outgoing, "head", split_axis=0, concat_axis=0, tiled=True)
    mine = jnp.transpose(incoming, (1, 2, 0, 3, 4)).reshape(2, 2, head_count * rows, width)
    qblocks = jnp.stack([device, count_of_blocks - 1 - device])
    pick_block = jnp.arange(count_of_blocks, dtype=jnp.int32)[None, :] == qblocks[:, None]
    plant_of = jnp.sum(jnp.where(pick_block, plant_ids[None, :], 0), axis=1)
    pick_plant = jnp.arange(layouts.shape[0], dtype=jnp.int32)[None, :] == plant_of[:, None]
    picked = pick_plant[:, :, None, None] & pick_block[:, None, :, None]
    listed_all = jnp.sum(jnp.where(picked, layouts[None], 0), axis=(1, 2))
    owners = jnp.where(listed_all < halfway, listed_all, count_of_blocks - 1 - listed_all)
    upper_half = (listed_all >= halfway).astype(jnp.int32)
    slot_of = jnp.where(owners == device, seq_count + upper_half, owners)
    live = jnp.stack([live_entries(listed_all[h]) for h in range(2)]).astype(jnp.int32)
    diagonal = (listed_all == qblocks[:, None]).astype(jnp.int32)
    flat_slots = slot_of.reshape(-1)
    flat_live = live.reshape(-1) != 0
    entry = jnp.arange(flat_slots.shape[0], dtype=jnp.int32)
    earlier_same = jnp.any(
        (flat_slots[None, :] == flat_slots[:, None]) & flat_live[None, :] & (entry[None, :] < entry[:, None]),
        axis=1,
    )
    first_touch = jnp.logical_not(earlier_same).astype(jnp.int32).reshape(2, -1)
    meta = jnp.stack([slot_of, live, first_touch], axis=1)
    dest = jnp.arange(seq_count, dtype=jnp.int32)
    send_lower = (dest >= device)[:, None, None, None]
    send = jnp.where(send_lower, mine[:, 0][None], mine[:, 1][None])
    received = lax.all_to_all(send, "seq", split_axis=0, concat_axis=0, tiled=True)
    outputs, query_grads, partials, own = attention_call(
        meta, queries, grad_out, received, mine, scaling
    )
    back = lax.all_to_all(partials, "seq", split_axis=0, concat_axis=0, tiled=True).astype(
        jnp.float32
    )
    source = jnp.arange(seq_count, dtype=jnp.int32)
    sender_blocks = jnp.stack([source, count_of_blocks - 1 - source], axis=1)
    sender_plants = plant_ids[sender_blocks]
    sender_lists = layouts[sender_plants, sender_blocks].reshape(seq_count, -1)
    wanted = jnp.where(source > device, device, count_of_blocks - 1 - device)
    listed_here = jnp.any(sender_lists == wanted[:, None], axis=1) & (source != device)
    from_higher = (listed_here & (source > device))[:, None, None, None]
    from_lower = (listed_here & (source < device))[:, None, None, None]
    lower_total = own[0] + jnp.sum(jnp.where(from_higher, back, 0.0), axis=0)
    upper_total = own[1] + jnp.sum(jnp.where(from_lower, back, 0.0), axis=0)
    totals = jnp.stack([lower_total, upper_total], axis=1).astype(jnp.bfloat16)
    outgoing = jnp.transpose(totals.reshape(2, 2, head_count, rows, width), (2, 0, 1, 3, 4))
    incoming = lax.all_to_all(outgoing, "head", split_axis=0, concat_axis=0, tiled=True)
    grads = jnp.transpose(incoming, (1, 2, 3, 0, 4)).reshape(2, 2, rows, head_count * width)
    return (outputs, query_grads, grads[0], grads[1])


def solution(mesh):
    in_specs = (
        P(None, "seq", "head"),
        P(None, ("seq", "head"), None),
        P(None, ("seq", "head"), None),
        P(None, "seq", "head"),
        P(),
        P(),
    )
    out_specs = (
        P(None, "seq", "head"),
        P(None, "seq", "head"),
        P(None, ("seq", "head"), None),
        P(None, ("seq", "head"), None),
    )
    return jax.shard_map(body, mesh=mesh, in_specs=in_specs, out_specs=out_specs, check_vma=False)
```
